256 devices in a mesh: gx: 16 (over z, core), gy: 16 (over x, y).
Axes of the slice: x: 4, y: 4, z: 8, core: 2. Of those that a mesh axis runs over, the one named last changes fastest.
Arguments:
- state: bfloat16 [2, 256, 768, 2048], P(None, None, 'gx', 'gy'), as said below
Outputs:
- modes: bfloat16 [255, 2, 768, 2048], P(None, None, 'gx', 'gy')
- reduced: float32 [255, 255], replicated
Inputs may be any that keep to these rules, and one draw needn't show every extreme that they name: `state`: both fields are positive.
All inputs are finite; a program needn't handle non-finite values.
Results may differ from the reference program's by a relative error of at most 0.0077.
Values may be sent and summed in bfloat16 or wider, within the bound.
No kernel may reach another device: no remote copies, remote signals or barrier semaphores. Data moves between devices by JAX's collectives and lax.ppermute only.
A program may use at most 128 MiB of HBM per device.

```python
import math
import jax
import jax.numpy as jnp
from jax import lax

SNAPS = 256
NX = 768
NY = 2048
ROWS = 3145728


def draw_state(key, part):
    key_w = jax.random.fold_in(key, 11)
    key_z = jax.random.fold_in(key, 12)
    key_d = jax.random.fold_in(key, 13)
    shared = 0.7 * jax.random.truncated_normal(key_w, -3.0, 3.0, (NX, NY), jnp.float32)
    own = 0.7 * jax.random.truncated_normal(key_z, -3.0, 3.0, (SNAPS, NX, NY), jnp.float32)
    noise = jax.random.truncated_normal(key_d, -3.0, 3.0, (SNAPS, NX, NY), jnp.float32)
    xpos = jnp.arange(NX, dtype=jnp.float32) / NX
    ypos = jnp.arange(NY, dtype=jnp.float32) / NY
    phase = jnp.arange(SNAPS, dtype=jnp.float32) * (2.0 / (SNAPS - 1)) - 1.0
    level = math.log(3.0) * (xpos[:, None] + ypos[None, :])
    tilt = 0.75 * (xpos[:, None] - ypos[None, :])
    logamp = level[None] + tilt[None] * phase[:, None, None]
    density = jnp.exp(0.3 * noise)
    energy = jnp.exp(logamp + shared[None] + own)
    return jnp.stack([density, energy]).astype(jnp.bfloat16)


def setup_inputs(seed: int = 0) -> dict:
    arg_keys = jax.random.split(jax.random.key(seed), 2)
    return {
        "state": draw_state(jax.random.fold_in(arg_keys[1], 71), 0),
    }


def tri_solve(lower, right):
    return lax.linalg.triangular_solve(lower, right, left_side=True, lower=True)

def gradients(temp):
    padded = jnp.pad(temp, 2)
    grad_x = (padded[:-4, 2:-2] - 8.0 * padded[1:-3, 2:-2] + 8.0 * padded[3:-1, 2:-2] - padded[4:, 2:-2]) / 12.0
    grad_y = (padded[2:-2, :-4] - 8.0 * padded[2:-2, 1:-3] + 8.0 * padded[2:-2, 3:-1] - padded[2:-2, 4:]) / 12.0
    return jnp.stack([grad_x, grad_y]).astype(jnp.bfloat16)

def one_snapshot(pair):
    density, energy = pair
    temp = 0.4 * energy.astype(jnp.float32) / density.astype(jnp.float32)
    return gradients(temp)

def reference(state):
    features = lax.map(one_snapshot, (state[0], state[1]))
    snap = features.reshape(SNAPS, ROWS)
    gram = lax.dot_general(snap.astype(jnp.float32), snap.astype(jnp.float32), (((1,), (1,)), ((), ())), preferred_element_type=jnp.float32) / ROWS
    lower = jnp.linalg.cholesky(gram[:SNAPS - 1, :SNAPS - 1])
    cross = gram[:SNAPS - 1, 1:]
    half = tri_solve(lower, cross)
    reduced = tri_solve(lower, half.T).T
    inverse = tri_solve(lower, jnp.eye(SNAPS - 1, dtype=jnp.float32)).astype(jnp.bfloat16)
    modes = jnp.dot(inverse.astype(jnp.float32), snap[1:].astype(jnp.float32), preferred_element_type=jnp.float32).astype(jnp.bfloat16)
    return (modes.reshape(SNAPS - 1, 2, NX, NY), reduced)
```

```python
import jax
import jax.numpy as jnp
from jax import lax
from jax.sharding import PartitionSpec as P


def padded_2(cells, sides, width):
    for axis, dim in sides:
        count = lax.axis_size(axis)
        ends = count - 1
        head = lax.slice_in_dim(cells, 0, width, axis=dim)
        tail = lax.slice_in_dim(cells, cells.shape[dim] - width, cells.shape[dim], axis=dim)
        cells = jnp.concatenate(
            [
                lax.ppermute(tail, axis, [(i, (i + 1) % count) for i in range(ends)]),
                cells,
                lax.ppermute(head, axis, [((i + 1) % count, i) for i in range(ends)]),
            ],
            axis=dim,
        )
    return cells


def pack_symmetric(gram):
    half = gram.shape[0] // 2
    upper_left = gram[:half, :half]
    lower_right = gram[half:, half:]
    rows = lax.broadcasted_iota(jnp.int32, (half, half), 0)
    cols = lax.broadcasted_iota(jnp.int32, (half, half), 1)
    folded = jnp.where(rows >= cols, upper_left, lower_right)
    return jnp.concatenate(
        [gram[half:, :half], folded, jnp.diagonal(lower_right)[None]], axis=0
    )


def unpack_symmetric(packed):
    half = packed.shape[1]
    block = packed[:half]
    folded = packed[half : 2 * half]
    diag = packed[2 * half]
    rows = lax.broadcasted_iota(jnp.int32, (half, half), 0)
    cols = lax.broadcasted_iota(jnp.int32, (half, half), 1)
    upper_left = jnp.where(rows >= cols, folded, folded.T)
    lower_right = jnp.where(rows < cols, folded, folded.T)
    lower_right = jnp.where(rows == cols, diag[None, :], lower_right)
    return jnp.concatenate(
        [
            jnp.concatenate([upper_left, block.T], axis=1),
            jnp.concatenate([block, lower_right], axis=1),
        ],
        axis=0,
    )


def doubling_sum(value, axis):
    count = lax.axis_size(axis)
    step = 1
    while step < count:
        value = value + lax.ppermute(value, axis, [(i, i ^ step) for i in range(count)])
        step *= 2
    return value


def tri_solve(lower, right):
    return lax.linalg.triangular_solve(lower, right, left_side=True, lower=True)


def gradients(padded):
    grad_x = (
        padded[:, :-4, 2:-2]
        - 8.0 * padded[:, 1:-3, 2:-2]
        + 8.0 * padded[:, 3:-1, 2:-2]
        - padded[:, 4:, 2:-2]
    ) / 12.0
    grad_y = (
        padded[:, 2:-2, :-4]
        - 8.0 * padded[:, 2:-2, 1:-3]
        + 8.0 * padded[:, 2:-2, 3:-1]
        - padded[:, 2:-2, 4:]
    ) / 12.0
    return jnp.stack([grad_x, grad_y], axis=1).astype(jnp.bfloat16)


def shards(state):
    snaps = state.shape[1]
    rows_x = state.shape[2]
    rows_y = state.shape[3]
    total_rows = 2 * rows_x * rows_y * lax.axis_size("gx") * lax.axis_size("gy")
    temp = 0.4 * state[1].astype(jnp.float32) / state[0].astype(jnp.float32)
    padded = padded_2(temp, (("gx", 1), ("gy", 2)), 2)
    features = gradients(padded)
    snap = features.reshape(snaps, 2 * rows_x * rows_y)
    local_gram = (
        lax.dot_general(snap, snap, (((1,), (1,)), ((), ())), preferred_element_type=jnp.float32)
        / total_rows
    )
    packed = doubling_sum(doubling_sum(pack_symmetric(local_gram), "gx"), "gy")
    gram = unpack_symmetric(packed)
    lower = jnp.linalg.cholesky(gram[: snaps - 1, : snaps - 1])
    cross = gram[: snaps - 1, 1:]
    half = tri_solve(lower, cross)
    reduced = tri_solve(lower, half.T).T
    inverse = tri_solve(lower, jnp.eye(snaps - 1, dtype=jnp.float32)).astype(jnp.bfloat16)
    modes = jnp.dot(inverse, snap[1:], preferred_element_type=jnp.float32).astype(jnp.bfloat16)
    return (modes.reshape(snaps - 1, 2, rows_x, rows_y), reduced)


def solution(mesh):
    placed = (P(None, None, "gx", "gy"),)
    return jax.shard_map(
        shards,
        mesh=mesh,
        in_specs=placed,
        out_specs=(P(None, None, "gx", "gy"), P()),
        check_vma=False,
    )
```

```python
import jax
import jax.numpy as jnp
from jax import lax
from jax.sharding import PartitionSpec as P


def padded_2(cells, sides, width):
    for axis, dim in sides:
        count = lax.axis_size(axis)
        ends = count - 1
        head = lax.slice_in_dim(cells, 0, width, axis=dim)
        tail = lax.slice_in_dim(cells, cells.shape[dim] - width, cells.shape[dim], axis=dim)
        cells = jnp.concatenate(
            [
                lax.ppermute(tail, axis, [(i, (i + 1) % count) for i in range(ends)]),
                cells,
                lax.ppermute(head, axis, [((i + 1) % count, i) for i in range(ends)]),
            ],
            axis=dim,
        )
    return cells


def pack_symmetric(gram):
    half = gram.shape[0] // 2
    upper_left = gram[:half, :half]
    lower_right = gram[half:, half:]
    rows = lax.broadcasted_iota(jnp.int32, (half, half), 0)
    cols = lax.broadcasted_iota(jnp.int32, (half, half), 1)
    folded = jnp.where(rows >= cols, upper_left, lower_right)
    return jnp.concatenate(
        [gram[half:, :half], folded, jnp.diagonal(lower_right)[None]], axis=0
    )


def unpack_symmetric(packed):
    half = packed.shape[1]
    block = packed[:half]
    folded = packed[half : 2 * half]
    diag = packed[2 * half]
    rows = lax.broadcasted_iota(jnp.int32, (half, half), 0)
    cols = lax.broadcasted_iota(jnp.int32, (half, half), 1)
    upper_left = jnp.where(rows >= cols, folded, folded.T)
    lower_right = jnp.where(rows < cols, folded, folded.T)
    lower_right = jnp.where(rows == cols, diag[None, :], lower_right)
    return jnp.concatenate(
        [
            jnp.concatenate([upper_left, block.T], axis=1),
            jnp.concatenate([block, lower_right], axis=1),
        ],
        axis=0,
    )


def doubling_sum(value, axis):
    count = lax.axis_size(axis)
    step = 1
    while step < count:
        value = value + lax.ppermute(value, axis, [(i, i ^ step) for i in range(count)])
        step *= 2
    return value


def tri_solve(lower, right):
    return lax.linalg.triangular_solve(lower, right, left_side=True, lower=True)


def gradients(padded):
    grad_x = (
        padded[:, :-4, 2:-2]
        - 8.0 * padded[:, 1:-3, 2:-2]
        + 8.0 * padded[:, 3:-1, 2:-2]
        - padded[:, 4:, 2:-2]
    ) / 12.0
    grad_y = (
        padded[:, 2:-2, :-4]
        - 8.0 * padded[:, 2:-2, 1:-3]
        + 8.0 * padded[:, 2:-2, 3:-1]
        - padded[:, 2:-2, 4:]
    ) / 12.0
    return jnp.stack([grad_x, grad_y], axis=1).astype(jnp.bfloat16)


def shards(state):
    snaps = state.shape[1]
    rows_x = state.shape[2]
    rows_y = state.shape[3]
    total_rows = 2 * rows_x * rows_y * lax.axis_size("gx") * lax.axis_size("gy")
    temp = 0.4 * state[1].astype(jnp.float32) / state[0].astype(jnp.float32)
    padded = padded_2(temp, (("gx", 1), ("gy", 2)), 2)
    features = gradients(padded)
    local_gram = (
        lax.dot_general(
            features, features, (((1, 2, 3), (1, 2, 3)), ((), ())), preferred_element_type=jnp.float32
        )
        / total_rows
    )
    packed = doubling_sum(doubling_sum(pack_symmetric(local_gram), "gx"), "gy")
    gram = unpack_symmetric(packed)
    lower = jnp.linalg.cholesky(gram[: snaps - 1, : snaps - 1])
    cross = gram[: snaps - 1, 1:]
    inverse = tri_solve(lower, jnp.eye(snaps - 1, dtype=jnp.float32))
    highest = lax.Precision.HIGHEST
    reduced = jnp.dot(jnp.dot(inverse, cross, precision=highest), inverse.T, precision=highest)
    shifted = jnp.concatenate(
        [jnp.zeros((snaps - 1, 1), jnp.bfloat16), inverse.astype(jnp.bfloat16)], axis=1
    )
    modes = lax.dot_general(
        shifted, features, (((1,), (0,)), ((), ())), preferred_element_type=jnp.float32
    ).astype(jnp.bfloat16)
    return (modes, reduced)


def solution(mesh):
    placed = (P(None, None, "gx", "gy"),)
    return jax.shard_map(
        shards,
        mesh=mesh,
        in_specs=placed,
        out_specs=(P(None, None, "gx", "gy"), P()),
        check_vma=False,
    )
```

```python
import jax
import jax.numpy as jnp
from jax import lax
from jax.experimental import pallas as pl
from jax.experimental.pallas import tpu as pltpu
from jax.sharding import PartitionSpec as P

BLOCK = 32


def feature_kernel(dens_ref, ener_ref, xh_ref, yh_ref, out_ref):
    nx = dens_ref.shape[2]
    ny = dens_ref.shape[3]
    rows = lax.broadcasted_iota(jnp.int32, (nx, ny), 0)
    cols = lax.broadcasted_iota(jnp.int32, (nx, ny), 1)

    def body(s, carry):
        temp = 0.4 * ener_ref[0, s].astype(jnp.float32) / dens_ref[0, s].astype(jnp.float32)
        xh = xh_ref[s]
        yh = yh_ref[s]
        up2 = jnp.where(rows == 0, xh[0:1], jnp.where(rows == 1, xh[1:2], pltpu.roll(temp, 2, 0)))
        up1 = jnp.where(rows == 0, xh[1:2], pltpu.roll(temp, 1, 0))
        dn1 = jnp.where(rows == nx - 1, xh[2:3], pltpu.roll(temp, nx - 1, 0))
        dn2 = jnp.where(rows == nx - 2, xh[2:3], jnp.where(rows == nx - 1, xh[3:4], pltpu.roll(temp, nx - 2, 0)))
        lf2 = jnp.where(cols == 0, yh[:, 0:1], jnp.where(cols == 1, yh[:, 1:2], pltpu.roll(temp, 2, 1)))
        lf1 = jnp.where(cols == 0, yh[:, 1:2], pltpu.roll(temp, 1, 1))
        rt1 = jnp.where(cols == ny - 1, yh[:, 2:3], pltpu.roll(temp, ny - 1, 1))
        rt2 = jnp.where(cols == ny - 2, yh[:, 2:3], jnp.where(cols == ny - 1, yh[:, 3:4], pltpu.roll(temp, ny - 2, 1)))
        grad_x = (up2 - 8.0 * up1 + 8.0 * dn1 - dn2) / 12.0
        grad_y = (lf2 - 8.0 * lf1 + 8.0 * rt1 - rt2) / 12.0
        out_ref[s, 0] = grad_x.astype(out_ref.dtype)
        out_ref[s, 1] = grad_y.astype(out_ref.dtype)
        return carry

    lax.fori_loop(0, dens_ref.shape[1], body, 0)


def features_of(state, xh, yh):
    _, snaps, nx, ny = state.shape
    block = min(BLOCK, snaps)
    return pl.pallas_call(
        feature_kernel,
        grid=(snaps // block,),
        in_specs=[
            pl.BlockSpec((1, block, nx, ny), lambda i: (0, i, 0, 0)),
            pl.BlockSpec((1, block, nx, ny), lambda i: (1, i, 0, 0)),
            pl.BlockSpec((block, 4, ny), lambda i: (i, 0, 0)),
            pl.BlockSpec((block, nx, 4), lambda i: (i, 0, 0)),
        ],
        out_specs=pl.BlockSpec((block, 2, nx, ny), lambda i: (i, 0, 0, 0)),
        out_shape=jax.ShapeDtypeStruct((snaps, 2, nx, ny), jnp.bfloat16),
    )(state, state, xh, yh)


def pack_symmetric(gram):
    half = gram.shape[0] // 2
    upper_left = gram[:half, :half]
    lower_right = gram[half:, half:]
    rows = lax.broadcasted_iota(jnp.int32, (half, half), 0)
    cols = lax.broadcasted_iota(jnp.int32, (half, half), 1)
    folded = jnp.where(rows >= cols, upper_left, lower_right)
    return jnp.concatenate(
        [gram[half:, :half], folded, jnp.diagonal(lower_right)[None]], axis=0
    )


def unpack_symmetric(packed):
    half = packed.shape[1]
    block = packed[:half]
    folded = packed[half : 2 * half]
    diag = packed[2 * half]
    rows = lax.broadcasted_iota(jnp.int32, (half, half), 0)
    cols = lax.broadcasted_iota(jnp.int32, (half, half), 1)
    upper_left = jnp.where(rows >= cols, folded, folded.T)
    lower_right = jnp.where(rows < cols, folded, folded.T)
    lower_right = jnp.where(rows == cols, diag[None, :], lower_right)
    return jnp.concatenate(
        [
            jnp.concatenate([upper_left, block.T], axis=1),
            jnp.concatenate([block, lower_right], axis=1),
        ],
        axis=0,
    )


def doubling_sum(value, axis):
    count = lax.axis_size(axis)
    step = 1
    while step < count:
        value = value + lax.ppermute(value, axis, [(i, i ^ step) for i in range(count)])
        step *= 2
    return value


def tri_solve(lower, right):
    return lax.linalg.triangular_solve(lower, right, left_side=True, lower=True)


def shards(state):
    snaps = state.shape[1]
    rows_x = state.shape[2]
    rows_y = state.shape[3]
    total_rows = 2 * rows_x * rows_y * lax.axis_size("gx") * lax.axis_size("gy")
    dens = state[0]
    ener = state[1]

    def temp_of(region):
        return 0.4 * ener[region].astype(jnp.float32) / dens[region].astype(jnp.float32)

    def shifted_pair(first, last, axis):
        count = lax.axis_size(axis)
        down = lax.ppermute(last, axis, [(i, i + 1) for i in range(count - 1)])
        up = lax.ppermute(first, axis, [(i + 1, i) for i in range(count - 1)])
        return down, up

    top, bottom = shifted_pair(
        temp_of((slice(None), slice(0, 2))), temp_of((slice(None), slice(rows_x - 2, rows_x))), "gx"
    )
    left, right = shifted_pair(
        temp_of((slice(None), slice(None), slice(0, 2))),
        temp_of((slice(None), slice(None), slice(rows_y - 2, rows_y))),
        "gy",
    )
    features = features_of(
        state, jnp.concatenate([top, bottom], axis=1), jnp.concatenate([left, right], axis=2)
    )
    local_gram = (
        lax.dot_general(
            features, features, (((1, 2, 3), (1, 2, 3)), ((), ())), preferred_element_type=jnp.float32
        )
        / total_rows
    )
    packed = doubling_sum(doubling_sum(pack_symmetric(local_gram), "gx"), "gy")
    gram = unpack_symmetric(packed)
    lower = jnp.linalg.cholesky(gram[: snaps - 1, : snaps - 1])
    cross = gram[: snaps - 1, 1:]
    inverse = tri_solve(lower, jnp.eye(snaps - 1, dtype=jnp.float32))
    highest = lax.Precision.HIGHEST
    reduced = jnp.dot(jnp.dot(inverse, cross, precision=highest), inverse.T, precision=highest)
    shifted = jnp.concatenate(
        [jnp.zeros((snaps - 1, 1), jnp.bfloat16), inverse.astype(jnp.bfloat16)], axis=1
    )
    modes = lax.dot_general(
        shifted, features, (((1,), (0,)), ((), ())), preferred_element_type=jnp.float32
    ).astype(jnp.bfloat16)
    return (modes, reduced)


def solution(mesh):
    placed = (P(None, None, "gx", "gy"),)
    return jax.shard_map(
        shards,
        mesh=mesh,
        in_specs=placed,
        out_specs=(P(None, None, "gx", "gy"), P()),
        check_vma=False,
    )
```

```python
import jax
import jax.numpy as jnp
from jax import lax
from jax.experimental import pallas as pl
from jax.experimental.pallas import tpu as pltpu
from jax.sharding import PartitionSpec as P

BLOCK = 32


def feature_kernel(dens_ref, ener_ref, xh_ref, yh_ref, out_ref):
    nx = dens_ref.shape[2]
    ny = dens_ref.shape[3]
    rows = lax.broadcasted_iota(jnp.int32, (nx, ny), 0)
    cols = lax.broadcasted_iota(jnp.int32, (nx, ny), 1)

    def body(s, carry):
        temp = 0.4 * ener_ref[0, s].astype(jnp.float32) / dens_ref[0, s].astype(jnp.float32)
        xh = xh_ref[s]
        yh = yh_ref[s]
        up2 = jnp.where(rows == 0, xh[0:1], jnp.where(rows == 1, xh[1:2], pltpu.roll(temp, 2, 0)))
        up1 = jnp.where(rows == 0, xh[1:2], pltpu.roll(temp, 1, 0))
        dn1 = jnp.where(rows == nx - 1, xh[2:3], pltpu.roll(temp, nx - 1, 0))
        dn2 = jnp.where(rows == nx - 2, xh[2:3], jnp.where(rows == nx - 1, xh[3:4], pltpu.roll(temp, nx - 2, 0)))
        lf2 = jnp.where(cols == 0, yh[:, 0:1], jnp.where(cols == 1, yh[:, 1:2], pltpu.roll(temp, 2, 1)))
        lf1 = jnp.where(cols == 0, yh[:, 1:2], pltpu.roll(temp, 1, 1))
        rt1 = jnp.where(cols == ny - 1, yh[:, 2:3], pltpu.roll(temp, ny - 1, 1))
        rt2 = jnp.where(cols == ny - 2, yh[:, 2:3], jnp.where(cols == ny - 1, yh[:, 3:4], pltpu.roll(temp, ny - 2, 1)))
        grad_x = (up2 - 8.0 * up1 + 8.0 * dn1 - dn2) / 12.0
        grad_y = (lf2 - 8.0 * lf1 + 8.0 * rt1 - rt2) / 12.0
        out_ref[s, 0] = grad_x.astype(out_ref.dtype)
        out_ref[s, 1] = grad_y.astype(out_ref.dtype)
        return carry

    lax.fori_loop(0, dens_ref.shape[1], body, 0, unroll=8)


def features_of(state, xh, yh):
    _, snaps, nx, ny = state.shape
    block = min(BLOCK, snaps)
    return pl.pallas_call(
        feature_kernel,
        grid=(snaps // block,),
        in_specs=[
            pl.BlockSpec((1, block, nx, ny), lambda i: (0, i, 0, 0)),
            pl.BlockSpec((1, block, nx, ny), lambda i: (1, i, 0, 0)),
            pl.BlockSpec((block, 4, ny), lambda i: (i, 0, 0)),
            pl.BlockSpec((block, nx, 4), lambda i: (i, 0, 0)),
        ],
        out_specs=pl.BlockSpec((block, 2, nx, ny), lambda i: (i, 0, 0, 0)),
        out_shape=jax.ShapeDtypeStruct((snaps, 2, nx, ny), jnp.bfloat16),
    )(state, state, xh, yh)


def pack_symmetric(gram):
    half = gram.shape[0] // 2
    upper_left = gram[:half, :half]
    lower_right = gram[half:, half:]
    rows = lax.broadcasted_iota(jnp.int32, (half, half), 0)
    cols = lax.broadcasted_iota(jnp.int32, (half, half), 1)
    folded = jnp.where(rows >= cols, upper_left, lower_right)
    return jnp.concatenate(
        [gram[half:, :half], folded, jnp.diagonal(lower_right)[None]], axis=0
    )


def unpack_symmetric(packed):
    half = packed.shape[1]
    block = packed[:half]
    folded = packed[half : 2 * half]
    diag = packed[2 * half]
    rows = lax.broadcasted_iota(jnp.int32, (half, half), 0)
    cols = lax.broadcasted_iota(jnp.int32, (half, half), 1)
    upper_left = jnp.where(rows >= cols, folded, folded.T)
    lower_right = jnp.where(rows < cols, folded, folded.T)
    lower_right = jnp.where(rows == cols, diag[None, :], lower_right)
    return jnp.concatenate(
        [
            jnp.concatenate([upper_left, block.T], axis=1),
            jnp.concatenate([block, lower_right], axis=1),
        ],
        axis=0,
    )


def doubling_sum(value, axis):
    count = lax.axis_size(axis)
    step = 1
    while step < count:
        value = value + lax.ppermute(value, axis, [(i, i ^ step) for i in range(count)])
        step *= 2
    return value


def tri_solve(lower, right):
    return lax.linalg.triangular_solve(lower, right, left_side=True, lower=True)


def shards(state):
    snaps = state.shape[1]
    rows_x = state.shape[2]
    rows_y = state.shape[3]
    total_rows = 2 * rows_x * rows_y * lax.axis_size("gx") * lax.axis_size("gy")
    dens = state[0]
    ener = state[1]

    def temp_of(region):
        return 0.4 * ener[region].astype(jnp.float32) / dens[region].astype(jnp.float32)

    def shifted_pair(first, last, axis):
        count = lax.axis_size(axis)
        down = lax.ppermute(last, axis, [(i, i + 1) for i in range(count - 1)])
        up = lax.ppermute(first, axis, [(i + 1, i) for i in range(count - 1)])
        return down, up

    top, bottom = shifted_pair(
        temp_of((slice(None), slice(0, 2))), temp_of((slice(None), slice(rows_x - 2, rows_x))), "gx"
    )
    left, right = shifted_pair(
        temp_of((slice(None), slice(None), slice(0, 2))),
        temp_of((slice(None), slice(None), slice(rows_y - 2, rows_y))),
        "gy",
    )
    features = features_of(
        state, jnp.concatenate([top, bottom], axis=1), jnp.concatenate([left, right], axis=2)
    )
    local_gram = (
        lax.dot_general(
            features, features, (((1, 2, 3), (1, 2, 3)), ((), ())), preferred_element_type=jnp.float32
        )
        / total_rows
    )
    packed = doubling_sum(doubling_sum(pack_symmetric(local_gram), "gx"), "gy")
    gram = unpack_symmetric(packed)
    lower = jnp.linalg.cholesky(gram[: snaps - 1, : snaps - 1])
    cross = gram[: snaps - 1, 1:]
    inverse = tri_solve(lower, jnp.eye(snaps - 1, dtype=jnp.float32))
    highest = lax.Precision.HIGHEST
    reduced = jnp.dot(jnp.dot(inverse, cross, precision=highest), inverse.T, precision=highest)
    shifted = jnp.concatenate(
        [jnp.zeros((snaps - 1, 1), jnp.bfloat16), inverse.astype(jnp.bfloat16)], axis=1
    )
    modes = lax.dot_general(
        shifted, features, (((1,), (0,)), ((), ())), preferred_element_type=jnp.float32
    ).astype(jnp.bfloat16)
    return (modes, reduced)


def solution(mesh):
    placed = (P(None, None, "gx", "gy"),)
    return jax.shard_map(
        shards,
        mesh=mesh,
        in_specs=placed,
        out_specs=(P(None, None, "gx", "gy"), P()),
        check_vma=False,
    )
```

```python
import jax
import jax.numpy as jnp
from jax import lax
from jax.experimental import pallas as pl
from jax.experimental.pallas import tpu as pltpu
from jax.sharding import PartitionSpec as P

BLOCK = 32


def feature_kernel(dens_ref, ener_ref, xh_ref, yh_ref, out_ref):
    nx = dens_ref.shape[2]
    ny = dens_ref.shape[3]
    lanes = yh_ref.shape[2]
    rows = lax.broadcasted_iota(jnp.int32, (nx, ny), 0)
    cols = lax.broadcasted_iota(jnp.int32, (nx, ny), 1)

    def body(s, carry):
        temp = 0.4 * ener_ref[0, s].astype(jnp.float32) / dens_ref[0, s].astype(jnp.float32)
        xh = xh_ref[s]
        halo = pltpu.roll(yh_ref[0], (ny - 2 - 4 * s) % lanes, 1)
        up2 = jnp.where(rows == 0, xh[0:1], jnp.where(rows == 1, xh[1:2], pltpu.roll(temp, 2, 0)))
        up1 = jnp.where(rows == 0, xh[1:2], pltpu.roll(temp, 1, 0))
        dn1 = jnp.where(rows == nx - 1, xh[2:3], pltpu.roll(temp, nx - 1, 0))
        dn2 = jnp.where(rows == nx - 2, xh[2:3], jnp.where(rows == nx - 1, xh[3:4], pltpu.roll(temp, nx - 2, 0)))
        lf2 = pltpu.roll(jnp.where(cols >= ny - 2, halo, temp), 2, 1)
        lf1 = pltpu.roll(jnp.where(cols == ny - 1, halo, temp), 1, 1)
        rt1 = pltpu.roll(jnp.where(cols == 0, halo, temp), ny - 1, 1)
        rt2 = pltpu.roll(jnp.where(cols < 2, halo, temp), ny - 2, 1)
        grad_x = (up2 - 8.0 * up1 + 8.0 * dn1 - dn2) / 12.0
        grad_y = (lf2 - 8.0 * lf1 + 8.0 * rt1 - rt2) / 12.0
        out_ref[s, 0] = grad_x.astype(out_ref.dtype)
        out_ref[s, 1] = grad_y.astype(out_ref.dtype)
        return carry

    lax.fori_loop(0, dens_ref.shape[1], body, 0, unroll=8)


def features_of(state, xh, yh):
    _, snaps, nx, ny = state.shape
    block = min(BLOCK, snaps)
    lanes = yh.shape[-1]
    return pl.pallas_call(
        feature_kernel,
        grid=(snaps // block,),
        in_specs=[
            pl.BlockSpec((1, block, nx, ny), lambda i: (0, i, 0, 0)),
            pl.BlockSpec((1, block, nx, ny), lambda i: (1, i, 0, 0)),
            pl.BlockSpec((block, 4, ny), lambda i: (i, 0, 0)),
            pl.BlockSpec((1, nx, lanes), lambda i: (i, 0, 0)),
        ],
        out_specs=pl.BlockSpec((block, 2, nx, ny), lambda i: (i, 0, 0, 0)),
        out_shape=jax.ShapeDtypeStruct((snaps, 2, nx, ny), jnp.bfloat16),
    )(state, state, xh, yh)


def regroup(yh):
    k, nx, snaps = yh.shape
    return yh.reshape(k, nx, snaps // BLOCK, BLOCK).transpose(2, 1, 3, 0).reshape(snaps // BLOCK, nx, k * BLOCK)


def pack_symmetric(gram):
    half = gram.shape[0] // 2
    upper_left = gram[:half, :half]
    lower_right = gram[half:, half:]
    rows = lax.broadcasted_iota(jnp.int32, (half, half), 0)
    cols = lax.broadcasted_iota(jnp.int32, (half, half), 1)
    folded = jnp.where(rows >= cols, upper_left, lower_right)
    return jnp.concatenate(
        [gram[half:, :half], folded, jnp.diagonal(lower_right)[None]], axis=0
    )


def unpack_symmetric(packed):
    half = packed.shape[1]
    block = packed[:half]
    folded = packed[half : 2 * half]
    diag = packed[2 * half]
    rows = lax.broadcasted_iota(jnp.int32, (half, half), 0)
    cols = lax.broadcasted_iota(jnp.int32, (half, half), 1)
    upper_left = jnp.where(rows >= cols, folded, folded.T)
    lower_right = jnp.where(rows < cols, folded, folded.T)
    lower_right = jnp.where(rows == cols, diag[None, :], lower_right)
    return jnp.concatenate(
        [
            jnp.concatenate([upper_left, block.T], axis=1),
            jnp.concatenate([block, lower_right], axis=1),
        ],
        axis=0,
    )


def doubling_sum(value, axis):
    count = lax.axis_size(axis)
    step = 1
    while step < count:
        value = value + lax.ppermute(value, axis, [(i, i ^ step) for i in range(count)])
        step *= 2
    return value


def tri_solve(lower, right):
    return lax.linalg.triangular_solve(lower, right, left_side=True, lower=True)


def shards(state):
    snaps = state.shape[1]
    rows_x = state.shape[2]
    rows_y = state.shape[3]
    total_rows = 2 * rows_x * rows_y * lax.axis_size("gx") * lax.axis_size("gy")
    def temp_of(region):
        return 0.4 * state[(1,) + region].astype(jnp.float32) / state[(0,) + region].astype(jnp.float32)

    def shifted_pair(first, last, axis):
        count = lax.axis_size(axis)
        down = lax.ppermute(last, axis, [(i, i + 1) for i in range(count - 1)])
        up = lax.ppermute(first, axis, [(i + 1, i) for i in range(count - 1)])
        return down, up

    every = slice(None)
    top, bottom = shifted_pair(
        temp_of((every, slice(0, 2))), temp_of((every, slice(rows_x - 2, rows_x))), "gx"
    )
    left, right = shifted_pair(
        jnp.transpose(temp_of((every, every, slice(0, 2))), (2, 1, 0)),
        jnp.transpose(temp_of((every, every, slice(rows_y - 2, rows_y))), (2, 1, 0)),
        "gy",
    )
    features = features_of(
        state,
        jnp.concatenate([top, bottom], axis=1),
        regroup(jnp.concatenate([left, right], axis=0)),
    )
    local_gram = (
        lax.dot_general(
            features, features, (((1, 2, 3), (1, 2, 3)), ((), ())), preferred_element_type=jnp.float32
        )
        / total_rows
    )
    packed = doubling_sum(doubling_sum(pack_symmetric(local_gram), "gx"), "gy")
    gram = unpack_symmetric(packed)
    lower = jnp.linalg.cholesky(gram[: snaps - 1, : snaps - 1])
    cross = gram[: snaps - 1, 1:]
    inverse = tri_solve(lower, jnp.eye(snaps - 1, dtype=jnp.float32))
    highest = lax.Precision.HIGHEST
    reduced = jnp.dot(jnp.dot(inverse, cross, precision=highest), inverse.T, precision=highest)
    shifted = jnp.concatenate(
        [jnp.zeros((snaps - 1, 1), jnp.bfloat16), inverse.astype(jnp.bfloat16)], axis=1
    )
    modes = lax.dot_general(
        shifted, features, (((1,), (0,)), ((), ())), preferred_element_type=jnp.float32
    ).astype(jnp.bfloat16)
    return (modes, reduced)


def solution(mesh):
    placed = (P(None, None, "gx", "gy"),)
    return jax.shard_map(
        shards,
        mesh=mesh,
        in_specs=placed,
        out_specs=(P(None, None, "gx", "gy"), P()),
        check_vma=False,
    )
```

```python
import jax
import jax.numpy as jnp
from jax import lax
from jax.experimental import pallas as pl
from jax.experimental.pallas import tpu as pltpu
from jax.sharding import PartitionSpec as P

BLOCK = 32


def feature_kernel(dens_ref, ener_ref, xh_ref, yh_ref, out_ref):
    nx = dens_ref.shape[2]
    ny = dens_ref.shape[3]
    lanes = yh_ref.shape[2]
    rows = lax.broadcasted_iota(jnp.int32, (nx, ny), 0)
    cols = lax.broadcasted_iota(jnp.int32, (nx, ny), 1)

    def body(s, carry):
        temp = 0.4 * ener_ref[0, s].astype(jnp.float32) / dens_ref[0, s].astype(jnp.float32)
        xh = xh_ref[s]
        halo = pltpu.roll(yh_ref[0], (ny - 2 - 4 * s) % lanes, 1)
        up2 = jnp.where(rows == 0, xh[0:1], jnp.where(rows == 1, xh[1:2], pltpu.roll(temp, 2, 0)))
        up1 = jnp.where(rows == 0, xh[1:2], pltpu.roll(temp, 1, 0))
        dn1 = jnp.where(rows == nx - 1, xh[2:3], pltpu.roll(temp, nx - 1, 0))
        dn2 = jnp.where(rows == nx - 2, xh[2:3], jnp.where(rows == nx - 1, xh[3:4], pltpu.roll(temp, nx - 2, 0)))
        lf2 = pltpu.roll(jnp.where(cols >= ny - 2, halo, temp), 2, 1)
        lf1 = pltpu.roll(jnp.where(cols == ny - 1, halo, temp), 1, 1)
        rt1 = pltpu.roll(jnp.where(cols == 0, halo, temp), ny - 1, 1)
        rt2 = pltpu.roll(jnp.where(cols < 2, halo, temp), ny - 2, 1)
        grad_x = (up2 - 8.0 * up1 + 8.0 * dn1 - dn2) / 12.0
        grad_y = (lf2 - 8.0 * lf1 + 8.0 * rt1 - rt2) / 12.0
        out_ref[s, 0] = grad_x.astype(out_ref.dtype)
        out_ref[s, 1] = grad_y.astype(out_ref.dtype)
        return carry

    lax.fori_loop(0, dens_ref.shape[1], body, 0, unroll=8)


def features_of(state, xh, yh):
    _, snaps, nx, ny = state.shape
    block = min(BLOCK, snaps)
    lanes = yh.shape[-1]
    return pl.pallas_call(
        feature_kernel,
        grid=(snaps // block,),
        in_specs=[
            pl.BlockSpec((1, block, nx, ny), lambda i: (0, i, 0, 0)),
            pl.BlockSpec((1, block, nx, ny), lambda i: (1, i, 0, 0)),
            pl.BlockSpec((block, 4, ny), lambda i: (i, 0, 0)),
            pl.BlockSpec((1, nx, lanes), lambda i: (i, 0, 0)),
        ],
        out_specs=pl.BlockSpec((block, 2, nx, ny), lambda i: (i, 0, 0, 0)),
        out_shape=jax.ShapeDtypeStruct((snaps, 2, nx, ny), jnp.bfloat16),
    )(state, state, xh, yh)


def edge_kernel(dens_ref, ener_ref, out_ref):
    nx = dens_ref.shape[2]
    ny = dens_ref.shape[3]
    group = lax.broadcasted_iota(jnp.int32, (nx, ny), 1) // 4

    def body(s, slab):
        temp = 0.4 * ener_ref[0, s].astype(jnp.float32) / dens_ref[0, s].astype(jnp.float32)
        return jnp.where(group == s, pltpu.roll(temp, (4 * s + 2) % ny, 1), slab)

    out_ref[0] = lax.fori_loop(0, dens_ref.shape[1], body, jnp.zeros((nx, ny), jnp.float32), unroll=8)


def edges_of(state):
    _, snaps, nx, ny = state.shape
    block = ny // 4
    return pl.pallas_call(
        edge_kernel,
        grid=(snaps // block,),
        in_specs=[
            pl.BlockSpec((1, block, nx, ny), lambda i: (0, i, 0, 0)),
            pl.BlockSpec((1, block, nx, ny), lambda i: (1, i, 0, 0)),
        ],
        out_specs=pl.BlockSpec((1, nx, ny), lambda i: (i, 0, 0)),
        out_shape=jax.ShapeDtypeStruct((snaps // block, nx, ny), jnp.float32),
    )(state, state)


def pack_symmetric(gram):
    half = gram.shape[0] // 2
    upper_left = gram[:half, :half]
    lower_right = gram[half:, half:]
    rows = lax.broadcasted_iota(jnp.int32, (half, half), 0)
    cols = lax.broadcasted_iota(jnp.int32, (half, half), 1)
    folded = jnp.where(rows >= cols, upper_left, lower_right)
    return jnp.concatenate(
        [gram[half:, :half], folded, jnp.diagonal(lower_right)[None]], axis=0
    )


def unpack_symmetric(packed):
    half = packed.shape[1]
    block = packed[:half]
    folded = packed[half : 2 * half]
    diag = packed[2 * half]
    rows = lax.broadcasted_iota(jnp.int32, (half, half), 0)
    cols = lax.broadcasted_iota(jnp.int32, (half, half), 1)
    upper_left = jnp.where(rows >= cols, folded, folded.T)
    lower_right = jnp.where(rows < cols, folded, folded.T)
    lower_right = jnp.where(rows == cols, diag[None, :], lower_right)
    return jnp.concatenate(
        [
            jnp.concatenate([upper_left, block.T], axis=1),
            jnp.concatenate([block, lower_right], axis=1),
        ],
        axis=0,
    )


def doubling_sum(value, axis):
    count = lax.axis_size(axis)
    step = 1
    while step < count:
        value = value + lax.ppermute(value, axis, [(i, i ^ step) for i in range(count)])
        step *= 2
    return value


def tri_solve(lower, right):
    return lax.linalg.triangular_solve(lower, right, left_side=True, lower=True)


def shards(state):
    snaps = state.shape[1]
    rows_x = state.shape[2]
    rows_y = state.shape[3]
    total_rows = 2 * rows_x * rows_y * lax.axis_size("gx") * lax.axis_size("gy")
    def temp_of(region):
        return 0.4 * state[(1,) + region].astype(jnp.float32) / state[(0,) + region].astype(jnp.float32)

    def shifted_pair(first, last, axis):
        count = lax.axis_size(axis)
        down = lax.ppermute(last, axis, [(i, i + 1) for i in range(count - 1)])
        up = lax.ppermute(first, axis, [(i + 1, i) for i in range(count - 1)])
        return down, up

    every = slice(None)
    top, bottom = shifted_pair(
        temp_of((every, slice(0, 2))), temp_of((every, slice(rows_x - 2, rows_x))), "gx"
    )
    slab = edges_of(state)
    count = lax.axis_size("gy")
    from_left = lax.ppermute(slab, "gy", [(i, i + 1) for i in range(count - 1)])
    from_right = lax.ppermute(slab, "gy", [(i + 1, i) for i in range(count - 1)])
    lane = lax.broadcasted_iota(jnp.int32, slab.shape, 2)
    features = features_of(
        state,
        jnp.concatenate([top, bottom], axis=1),
        jnp.where(lane % 4 < 2, from_left, from_right),
    )
    local_gram = (
        lax.dot_general(
            features, features, (((1, 2, 3), (1, 2, 3)), ((), ())), preferred_element_type=jnp.float32
        )
        / total_rows
    )
    packed = doubling_sum(doubling_sum(pack_symmetric(local_gram), "gx"), "gy")
    gram = unpack_symmetric(packed)
    lower = jnp.linalg.cholesky(gram[: snaps - 1, : snaps - 1])
    cross = gram[: snaps - 1, 1:]
    inverse = tri_solve(lower, jnp.eye(snaps - 1, dtype=jnp.float32))
    highest = lax.Precision.HIGHEST
    reduced = jnp.dot(jnp.dot(inverse, cross, precision=highest), inverse.T, precision=highest)
    shifted = jnp.concatenate(
        [jnp.zeros((snaps - 1, 1), jnp.bfloat16), inverse.astype(jnp.bfloat16)], axis=1
    )
    modes = lax.dot_general(
        shifted, features, (((1,), (0,)), ((), ())), preferred_element_type=jnp.float32
    ).astype(jnp.bfloat16)
    return (modes, reduced)


def solution(mesh):
    placed = (P(None, None, "gx", "gy"),)
    return jax.shard_map(
        shards,
        mesh=mesh,
        in_specs=placed,
        out_specs=(P(None, None, "gx", "gy"), P()),
        check_vma=False,
    )
```

```python
import numpy as np
import jax
import jax.numpy as jnp
from jax import lax
from jax.experimental import pallas as pl
from jax.experimental.pallas import tpu as pltpu
from jax.sharding import PartitionSpec as P

BLOCK = 32


def feature_kernel(dens_ref, ener_ref, xh_ref, yh_ref, out_ref):
    nx = dens_ref.shape[2]
    ny = dens_ref.shape[3]
    lanes = yh_ref.shape[2]
    rows = lax.broadcasted_iota(jnp.int32, (nx, ny), 0)
    cols = lax.broadcasted_iota(jnp.int32, (nx, ny), 1)

    def body(s, carry):
        temp = 0.4 * ener_ref[0, s].astype(jnp.float32) / dens_ref[0, s].astype(jnp.float32)
        xh = xh_ref[s]
        halo = pltpu.roll(yh_ref[0], (ny - 2 - 4 * s) % lanes, 1)
        up2 = jnp.where(rows == 0, xh[0:1], jnp.where(rows == 1, xh[1:2], pltpu.roll(temp, 2, 0)))
        up1 = jnp.where(rows == 0, xh[1:2], pltpu.roll(temp, 1, 0))
        dn1 = jnp.where(rows == nx - 1, xh[2:3], pltpu.roll(temp, nx - 1, 0))
        dn2 = jnp.where(rows == nx - 2, xh[2:3], jnp.where(rows == nx - 1, xh[3:4], pltpu.roll(temp, nx - 2, 0)))
        lf2 = pltpu.roll(jnp.where(cols >= ny - 2, halo, temp), 2, 1)
        lf1 = pltpu.roll(jnp.where(cols == ny - 1, halo, temp), 1, 1)
        rt1 = pltpu.roll(jnp.where(cols == 0, halo, temp), ny - 1, 1)
        rt2 = pltpu.roll(jnp.where(cols < 2, halo, temp), ny - 2, 1)
        grad_x = (up2 - 8.0 * up1 + 8.0 * dn1 - dn2) / 12.0
        grad_y = (lf2 - 8.0 * lf1 + 8.0 * rt1 - rt2) / 12.0
        out_ref[s, 0] = grad_x.astype(out_ref.dtype)
        out_ref[s, 1] = grad_y.astype(out_ref.dtype)
        return carry

    lax.fori_loop(0, dens_ref.shape[1], body, 0, unroll=8)


def features_of(state, xh, yh):
    _, snaps, nx, ny = state.shape
    block = min(BLOCK, snaps)
    lanes = yh.shape[-1]
    return pl.pallas_call(
        feature_kernel,
        grid=(snaps // block,),
        in_specs=[
            pl.BlockSpec((1, block, nx, ny), lambda i: (0, i, 0, 0)),
            pl.BlockSpec((1, block, nx, ny), lambda i: (1, i, 0, 0)),
            pl.BlockSpec((block, 4, ny), lambda i: (i, 0, 0)),
            pl.BlockSpec((1, nx, lanes), lambda i: (i, 0, 0)),
        ],
        out_specs=pl.BlockSpec((block, 2, nx, ny), lambda i: (i, 0, 0, 0)),
        out_shape=jax.ShapeDtypeStruct((snaps, 2, nx, ny), jnp.bfloat16),
    )(state, state, xh, yh)


def edge_kernel(dens_ref, ener_ref, out_ref):
    nx = dens_ref.shape[2]
    ny = dens_ref.shape[3]
    group = lax.broadcasted_iota(jnp.int32, (nx, ny), 1) // 4

    def body(s, slab):
        temp = 0.4 * ener_ref[0, s].astype(jnp.float32) / dens_ref[0, s].astype(jnp.float32)
        return jnp.where(group == s, pltpu.roll(temp, (4 * s + 2) % ny, 1), slab)

    out_ref[0] = lax.fori_loop(0, dens_ref.shape[1], body, jnp.zeros((nx, ny), jnp.float32), unroll=8)


def edges_of(state):
    _, snaps, nx, ny = state.shape
    block = ny // 4
    return pl.pallas_call(
        edge_kernel,
        grid=(snaps // block,),
        in_specs=[
            pl.BlockSpec((1, block, nx, ny), lambda i: (0, i, 0, 0)),
            pl.BlockSpec((1, block, nx, ny), lambda i: (1, i, 0, 0)),
        ],
        out_specs=pl.BlockSpec((1, nx, ny), lambda i: (i, 0, 0)),
        out_shape=jax.ShapeDtypeStruct((snaps // block, nx, ny), jnp.float32),
    )(state, state)


def pack_symmetric(gram):
    half = gram.shape[0] // 2
    upper_left = gram[:half, :half]
    lower_right = gram[half:, half:]
    rows = lax.broadcasted_iota(jnp.int32, (half, half), 0)
    cols = lax.broadcasted_iota(jnp.int32, (half, half), 1)
    folded = jnp.where(rows >= cols, upper_left, lower_right)
    return jnp.concatenate(
        [gram[half:, :half], folded, jnp.diagonal(lower_right)[None]], axis=0
    )


def unpack_symmetric(packed):
    half = packed.shape[1]
    block = packed[:half]
    folded = packed[half : 2 * half]
    diag = packed[2 * half]
    rows = lax.broadcasted_iota(jnp.int32, (half, half), 0)
    cols = lax.broadcasted_iota(jnp.int32, (half, half), 1)
    upper_left = jnp.where(rows >= cols, folded, folded.T)
    lower_right = jnp.where(rows < cols, folded, folded.T)
    lower_right = jnp.where(rows == cols, diag[None, :], lower_right)
    return jnp.concatenate(
        [
            jnp.concatenate([upper_left, block.T], axis=1),
            jnp.concatenate([block, lower_right], axis=1),
        ],
        axis=0,
    )


def lower_slots(rows, cols, width):
    taken = [(i, j) for i in range(rows) for j in range(cols) if j <= i]
    flat = np.array([i * cols + j for i, j in taken], np.int32)
    length = -(-len(flat) // width) * width
    picks = np.zeros(length, np.int32)
    picks[: len(flat)] = flat
    spot = {pair: n for n, pair in enumerate(taken)}
    back = np.array([[spot[max(i, j), min(i, j)] for j in range(cols)] for i in range(rows)], np.int32)
    return picks, back


def pack_lower(block, width):
    picks, _ = lower_slots(block.shape[0], block.shape[1], width)
    return block.reshape(-1)[picks].reshape(-1, width)


def unpack_lower(packed, size):
    _, back = lower_slots(size, size, packed.shape[1])
    return packed.reshape(-1)[back]


def doubling_sum(value, axis):
    count = lax.axis_size(axis)
    step = 1
    while step < count:
        value = value + lax.ppermute(value, axis, [(i, i ^ step) for i in range(count)])
        step *= 2
    return value


def tri_solve(lower, right):
    return lax.linalg.triangular_solve(lower, right, left_side=True, lower=True)


def shards(state):
    snaps = state.shape[1]
    rows_x = state.shape[2]
    rows_y = state.shape[3]
    total_rows = 2 * rows_x * rows_y * lax.axis_size("gx") * lax.axis_size("gy")
    def temp_of(region):
        return 0.4 * state[(1,) + region].astype(jnp.float32) / state[(0,) + region].astype(jnp.float32)

    def shifted_pair(first, last, axis):
        count = lax.axis_size(axis)
        down = lax.ppermute(last, axis, [(i, i + 1) for i in range(count - 1)])
        up = lax.ppermute(first, axis, [(i + 1, i) for i in range(count - 1)])
        return down, up

    every = slice(None)
    top, bottom = shifted_pair(
        temp_of((every, slice(0, 2))), temp_of((every, slice(rows_x - 2, rows_x))), "gx"
    )
    slab = edges_of(state)
    count = lax.axis_size("gy")
    from_left = lax.ppermute(slab, "gy", [(i, i + 1) for i in range(count - 1)])
    from_right = lax.ppermute(slab, "gy", [(i + 1, i) for i in range(count - 1)])
    lane = lax.broadcasted_iota(jnp.int32, slab.shape, 2)
    features = features_of(
        state,
        jnp.concatenate([top, bottom], axis=1),
        jnp.where(lane % 4 < 2, from_left, from_right),
    )
    local_gram = (
        lax.dot_general(
            features, features, (((1, 2, 3), (1, 2, 3)), ((), ())), preferred_element_type=jnp.float32
        )
        / total_rows
    )
    half = snaps // 2
    lead = unpack_lower(
        doubling_sum(doubling_sum(pack_lower(local_gram[:half, :half], half), "gx"), "gy"), half
    )
    rest = doubling_sum(
        doubling_sum(
            jnp.concatenate(
                [local_gram[half:, :half], pack_lower(local_gram[half:, half:], half)], axis=0
            ),
            "gx",
        ),
        "gy",
    )
    side = rest[:half]
    corner = unpack_lower(rest[half:], half)
    gram = jnp.concatenate(
        [jnp.concatenate([lead, side.T], axis=1), jnp.concatenate([side, corner], axis=1)], axis=0
    )
    highest = lax.Precision.HIGHEST
    size = snaps - 1
    low11 = jnp.linalg.cholesky(lead)
    inv11 = tri_solve(low11, jnp.eye(half, dtype=jnp.float32))
    low21 = jnp.dot(side[: size - half], inv11.T, precision=highest)
    schur = corner[: size - half, : size - half] - jnp.dot(low21, low21.T, precision=highest)
    low22 = jnp.linalg.cholesky(schur)
    inv22 = tri_solve(low22, jnp.eye(size - half, dtype=jnp.float32))
    inv21 = -jnp.dot(inv22, jnp.dot(low21, inv11, precision=highest), precision=highest)
    inverse = jnp.concatenate(
        [
            jnp.concatenate([inv11, jnp.zeros((half, size - half), jnp.float32)], axis=1),
            jnp.concatenate([inv21, inv22], axis=1),
        ],
        axis=0,
    )
    cross = gram[:size, 1:]
    reduced = jnp.dot(jnp.dot(inverse, cross, precision=highest), inverse.T, precision=highest)
    shifted = jnp.concatenate(
        [jnp.zeros((snaps - 1, 1), jnp.bfloat16), inverse.astype(jnp.bfloat16)], axis=1
    )
    modes = lax.dot_general(
        shifted, features, (((1,), (0,)), ((), ())), preferred_element_type=jnp.float32
    ).astype(jnp.bfloat16)
    return (modes, reduced)


def solution(mesh):
    placed = (P(None, None, "gx", "gy"),)
    return jax.shard_map(
        shards,
        mesh=mesh,
        in_specs=placed,
        out_specs=(P(None, None, "gx", "gy"), P()),
        check_vma=False,
    )
```

```python
import jax
import jax.numpy as jnp
from jax import lax
from jax.experimental import pallas as pl
from jax.experimental.pallas import tpu as pltpu
from jax.sharding import PartitionSpec as P

BLOCK = 32


def feature_kernel(dens_ref, ener_ref, xh_ref, yh_ref, out_ref):
    nx = dens_ref.shape[2]
    ny = dens_ref.shape[3]
    lanes = yh_ref.shape[2]
    rows = lax.broadcasted_iota(jnp.int32, (nx, ny), 0)
    cols = lax.broadcasted_iota(jnp.int32, (nx, ny), 1)

    def body(s, carry):
        temp = 0.4 * ener_ref[0, s].astype(jnp.float32) / dens_ref[0, s].astype(jnp.float32)
        xh = xh_ref[s]
        halo = pltpu.roll(yh_ref[0], (ny - 2 - 4 * s) % lanes, 1)
        up2 = jnp.where(rows == 0, xh[0:1], jnp.where(rows == 1, xh[1:2], pltpu.roll(temp, 2, 0)))
        up1 = jnp.where(rows == 0, xh[1:2], pltpu.roll(temp, 1, 0))
        dn1 = jnp.where(rows == nx - 1, xh[2:3], pltpu.roll(temp, nx - 1, 0))
        dn2 = jnp.where(rows == nx - 2, xh[2:3], jnp.where(rows == nx - 1, xh[3:4], pltpu.roll(temp, nx - 2, 0)))
        lf2 = pltpu.roll(jnp.where(cols >= ny - 2, halo, temp), 2, 1)
        lf1 = pltpu.roll(jnp.where(cols == ny - 1, halo, temp), 1, 1)
        rt1 = pltpu.roll(jnp.where(cols == 0, halo, temp), ny - 1, 1)
        rt2 = pltpu.roll(jnp.where(cols < 2, halo, temp), ny - 2, 1)
        grad_x = (up2 - 8.0 * up1 + 8.0 * dn1 - dn2) / 12.0
        grad_y = (lf2 - 8.0 * lf1 + 8.0 * rt1 - rt2) / 12.0
        out_ref[s, 0] = grad_x.astype(out_ref.dtype)
        out_ref[s, 1] = grad_y.astype(out_ref.dtype)
        return carry

    lax.fori_loop(0, dens_ref.shape[1], body, 0, unroll=8)


def features_of(state, xh, yh):
    _, snaps, nx, ny = state.shape
    block = min(BLOCK, snaps)
    lanes = yh.shape[-1]
    return pl.pallas_call(
        feature_kernel,
        grid=(snaps // block,),
        in_specs=[
            pl.BlockSpec((1, block, nx, ny), lambda i: (0, i, 0, 0)),
            pl.BlockSpec((1, block, nx, ny), lambda i: (1, i, 0, 0)),
            pl.BlockSpec((block, 4, ny), lambda i: (i, 0, 0)),
            pl.BlockSpec((1, nx, lanes), lambda i: (i, 0, 0)),
        ],
        out_specs=pl.BlockSpec((block, 2, nx, ny), lambda i: (i, 0, 0, 0)),
        out_shape=jax.ShapeDtypeStruct((snaps, 2, nx, ny), jnp.bfloat16),
    )(state, state, xh, yh)


def edge_kernel(dens_ref, ener_ref, out_ref):
    nx = dens_ref.shape[2]
    ny = dens_ref.shape[3]
    group = lax.broadcasted_iota(jnp.int32, (nx, ny), 1) // 4

    def body(s, slab):
        temp = 0.4 * ener_ref[0, s].astype(jnp.float32) / dens_ref[0, s].astype(jnp.float32)
        return jnp.where(group == s, pltpu.roll(temp, (4 * s + 2) % ny, 1), slab)

    out_ref[0] = lax.fori_loop(0, dens_ref.shape[1], body, jnp.zeros((nx, ny), jnp.float32), unroll=8)


def edges_of(state):
    _, snaps, nx, ny = state.shape
    block = ny // 4
    return pl.pallas_call(
        edge_kernel,
        grid=(snaps // block,),
        in_specs=[
            pl.BlockSpec((1, block, nx, ny), lambda i: (0, i, 0, 0)),
            pl.BlockSpec((1, block, nx, ny), lambda i: (1, i, 0, 0)),
        ],
        out_specs=pl.BlockSpec((1, nx, ny), lambda i: (i, 0, 0)),
        out_shape=jax.ShapeDtypeStruct((snaps // block, nx, ny), jnp.float32),
    )(state, state)


def pack_symmetric(gram):
    half = gram.shape[0] // 2
    upper_left = gram[:half, :half]
    lower_right = gram[half:, half:]
    rows = lax.broadcasted_iota(jnp.int32, (half, half), 0)
    cols = lax.broadcasted_iota(jnp.int32, (half, half), 1)
    folded = jnp.where(rows >= cols, upper_left, lower_right)
    return jnp.concatenate(
        [gram[half:, :half], folded, jnp.diagonal(lower_right)[None]], axis=0
    )


def unpack_symmetric(packed):
    half = packed.shape[1]
    block = packed[:half]
    folded = packed[half : 2 * half]
    diag = packed[2 * half]
    rows = lax.broadcasted_iota(jnp.int32, (half, half), 0)
    cols = lax.broadcasted_iota(jnp.int32, (half, half), 1)
    upper_left = jnp.where(rows >= cols, folded, folded.T)
    lower_right = jnp.where(rows < cols, folded, folded.T)
    lower_right = jnp.where(rows == cols, diag[None, :], lower_right)
    return jnp.concatenate(
        [
            jnp.concatenate([upper_left, block.T], axis=1),
            jnp.concatenate([block, lower_right], axis=1),
        ],
        axis=0,
    )


def doubling_sum(value, axis):
    count = lax.axis_size(axis)
    step = 1
    while step < count:
        value = value + lax.ppermute(value, axis, [(i, i ^ step) for i in range(count)])
        step *= 2
    return value


def tri_solve(lower, right):
    return lax.linalg.triangular_solve(lower, right, left_side=True, lower=True)


def shards(state):
    snaps = state.shape[1]
    rows_x = state.shape[2]
    rows_y = state.shape[3]
    total_rows = 2 * rows_x * rows_y * lax.axis_size("gx") * lax.axis_size("gy")
    def temp_of(region):
        return 0.4 * state[(1,) + region].astype(jnp.float32) / state[(0,) + region].astype(jnp.float32)

    def shifted_pair(first, last, axis):
        count = lax.axis_size(axis)
        down = lax.ppermute(last, axis, [(i, i + 1) for i in range(count - 1)])
        up = lax.ppermute(first, axis, [(i + 1, i) for i in range(count - 1)])
        return down, up

    every = slice(None)
    top, bottom = shifted_pair(
        temp_of((every, slice(0, 2))), temp_of((every, slice(rows_x - 2, rows_x))), "gx"
    )
    slab = edges_of(state)
    count = lax.axis_size("gy")
    from_left = lax.ppermute(slab, "gy", [(i, i + 1) for i in range(count - 1)])
    from_right = lax.ppermute(slab, "gy", [(i + 1, i) for i in range(count - 1)])
    lane = lax.broadcasted_iota(jnp.int32, slab.shape, 2)
    features = features_of(
        state,
        jnp.concatenate([top, bottom], axis=1),
        jnp.where(lane % 4 < 2, from_left, from_right),
    )
    local_gram = (
        lax.dot_general(
            features, features, (((1, 2, 3), (1, 2, 3)), ((), ())), preferred_element_type=jnp.float32
        )
        / total_rows
    )
    half = snaps // 2
    packed = pack_symmetric(local_gram)
    folded = doubling_sum(doubling_sum(packed[half : 2 * half], "gx"), "gy")
    edge = jnp.concatenate([packed[:half], packed[2 * half :]], axis=0)
    edge = doubling_sum(doubling_sum(edge, "gx"), "gy")
    side = edge[:half]
    gram = unpack_symmetric(jnp.concatenate([side, folded, edge[half:]], axis=0))
    lead = gram[:half, :half]
    corner = gram[half:, half:]
    highest = lax.Precision.HIGHEST
    size = snaps - 1
    low11 = jnp.linalg.cholesky(lead)
    inv11 = tri_solve(low11, jnp.eye(half, dtype=jnp.float32))
    low21 = jnp.dot(side[: size - half], inv11.T, precision=highest)
    schur = corner[: size - half, : size - half] - jnp.dot(low21, low21.T, precision=highest)
    low22 = jnp.linalg.cholesky(schur)
    inv22 = tri_solve(low22, jnp.eye(size - half, dtype=jnp.float32))
    inv21 = -jnp.dot(inv22, jnp.dot(low21, inv11, precision=highest), precision=highest)
    inverse = jnp.concatenate(
        [
            jnp.concatenate([inv11, jnp.zeros((half, size - half), jnp.float32)], axis=1),
            jnp.concatenate([inv21, inv22], axis=1),
        ],
        axis=0,
    )
    cross = gram[:size, 1:]
    reduced = jnp.dot(jnp.dot(inverse, cross, precision=highest), inverse.T, precision=highest)
    shifted = jnp.concatenate(
        [jnp.zeros((snaps - 1, 1), jnp.bfloat16), inverse.astype(jnp.bfloat16)], axis=1
    )
    modes = lax.dot_general(
        shifted, features, (((1,), (0,)), ((), ())), preferred_element_type=jnp.float32
    ).astype(jnp.bfloat16)
    return (modes, reduced)


def solution(mesh):
    placed = (P(None, None, "gx", "gy"),)
    return jax.shard_map(
        shards,
        mesh=mesh,
        in_specs=placed,
        out_specs=(P(None, None, "gx", "gy"), P()),
        check_vma=False,
    )
```

```python
import jax
import jax.numpy as jnp
from jax import lax
from jax.experimental import pallas as pl
from jax.experimental.pallas import tpu as pltpu
from jax.sharding import PartitionSpec as P

BLOCK = 32


def feature_kernel(dens_ref, ener_ref, xh_ref, yh_ref, out_ref):
    nx = dens_ref.shape[2]
    ny = dens_ref.shape[3]
    lanes = yh_ref.shape[2]
    rows = lax.broadcasted_iota(jnp.int32, (nx, ny), 0)
    cols = lax.broadcasted_iota(jnp.int32, (nx, ny), 1)

    def body(s, carry):
        temp = 0.4 * ener_ref[0, s].astype(jnp.float32) / dens_ref[0, s].astype(jnp.float32)
        xh = xh_ref[s]
        halo = pltpu.roll(yh_ref[0], (ny - 2 - 4 * s) % lanes, 1)
        up2 = jnp.where(rows == 0, xh[0:1], jnp.where(rows == 1, xh[1:2], pltpu.roll(temp, 2, 0)))
        up1 = jnp.where(rows == 0, xh[1:2], pltpu.roll(temp, 1, 0))
        dn1 = jnp.where(rows == nx - 1, xh[2:3], pltpu.roll(temp, nx - 1, 0))
        dn2 = jnp.where(rows == nx - 2, xh[2:3], jnp.where(rows == nx - 1, xh[3:4], pltpu.roll(temp, nx - 2, 0)))
        lf2 = pltpu.roll(jnp.where(cols >= ny - 2, halo, temp), 2, 1)
        lf1 = pltpu.roll(jnp.where(cols == ny - 1, halo, temp), 1, 1)
        rt1 = pltpu.roll(jnp.where(cols == 0, halo, temp), ny - 1, 1)
        rt2 = pltpu.roll(jnp.where(cols < 2, halo, temp), ny - 2, 1)
        grad_x = (up2 - 8.0 * up1 + 8.0 * dn1 - dn2) / 12.0
        grad_y = (lf2 - 8.0 * lf1 + 8.0 * rt1 - rt2) / 12.0
        out_ref[s, 0] = grad_x.astype(out_ref.dtype)
        out_ref[s, 1] = grad_y.astype(out_ref.dtype)
        return carry

    lax.fori_loop(0, dens_ref.shape[1], body, 0, unroll=8)


def features_of(state, xh, yh, part, parts, into=None):
    _, snaps, nx, ny = state.shape
    block = min(BLOCK, snaps)
    lanes = yh.shape[-1]
    steps = snaps // block // parts
    first = part * steps
    specs = [
        pl.BlockSpec((1, block, nx, ny), lambda i: (0, i + first, 0, 0)),
        pl.BlockSpec((1, block, nx, ny), lambda i: (1, i + first, 0, 0)),
        pl.BlockSpec((block, 4, ny), lambda i: (i + first, 0, 0)),
        pl.BlockSpec((1, nx, lanes), lambda i: (i + first, 0, 0)),
    ]
    operands = [state, state, xh, yh]
    aliases = {}
    kernel = feature_kernel
    if into is not None:
        specs.append(pl.BlockSpec(memory_space=pl.ANY))
        operands.append(into)
        aliases = {4: 0}

        def kernel(dens_ref, ener_ref, xh_ref, yh_ref, into_ref, out_ref):
            feature_kernel(dens_ref, ener_ref, xh_ref, yh_ref, out_ref)

    return pl.pallas_call(
        kernel,
        grid=(steps,),
        in_specs=specs,
        out_specs=pl.BlockSpec((block, 2, nx, ny), lambda i: (i + first, 0, 0, 0)),
        out_shape=jax.ShapeDtypeStruct((snaps, 2, nx, ny), jnp.bfloat16),
        input_output_aliases=aliases,
    )(*operands)


def edge_kernel(dens_ref, ener_ref, out_ref):
    nx = dens_ref.shape[2]
    ny = dens_ref.shape[3]
    group = lax.broadcasted_iota(jnp.int32, (nx, ny), 1) // 4

    def body(s, slab):
        temp = 0.4 * ener_ref[0, s].astype(jnp.float32) / dens_ref[0, s].astype(jnp.float32)
        return jnp.where(group == s, pltpu.roll(temp, (4 * s + 2) % ny, 1), slab)

    out_ref[0] = lax.fori_loop(0, dens_ref.shape[1], body, jnp.zeros((nx, ny), jnp.float32), unroll=8)


def edges_of(state):
    _, snaps, nx, ny = state.shape
    block = ny // 4
    return pl.pallas_call(
        edge_kernel,
        grid=(snaps // block,),
        in_specs=[
            pl.BlockSpec((1, block, nx, ny), lambda i: (0, i, 0, 0)),
            pl.BlockSpec((1, block, nx, ny), lambda i: (1, i, 0, 0)),
        ],
        out_specs=pl.BlockSpec((1, nx, ny), lambda i: (i, 0, 0)),
        out_shape=jax.ShapeDtypeStruct((snaps // block, nx, ny), jnp.float32),
    )(state, state)


def pack_symmetric(gram):
    half = gram.shape[0] // 2
    upper_left = gram[:half, :half]
    lower_right = gram[half:, half:]
    rows = lax.broadcasted_iota(jnp.int32, (half, half), 0)
    cols = lax.broadcasted_iota(jnp.int32, (half, half), 1)
    folded = jnp.where(rows >= cols, upper_left, lower_right)
    return jnp.concatenate(
        [gram[half:, :half], folded, jnp.diagonal(lower_right)[None]], axis=0
    )


def unpack_symmetric(packed):
    half = packed.shape[1]
    block = packed[:half]
    folded = packed[half : 2 * half]
    diag = packed[2 * half]
    rows = lax.broadcasted_iota(jnp.int32, (half, half), 0)
    cols = lax.broadcasted_iota(jnp.int32, (half, half), 1)
    upper_left = jnp.where(rows >= cols, folded, folded.T)
    lower_right = jnp.where(rows < cols, folded, folded.T)
    lower_right = jnp.where(rows == cols, diag[None, :], lower_right)
    return jnp.concatenate(
        [
            jnp.concatenate([upper_left, block.T], axis=1),
            jnp.concatenate([block, lower_right], axis=1),
        ],
        axis=0,
    )


def doubling_sum(value, axis):
    count = lax.axis_size(axis)
    step = 1
    while step < count:
        value = value + lax.ppermute(value, axis, [(i, i ^ step) for i in range(count)])
        step *= 2
    return value


def tri_solve(lower, right):
    return lax.linalg.triangular_solve(lower, right, left_side=True, lower=True)


def shards(state):
    snaps = state.shape[1]
    rows_x = state.shape[2]
    rows_y = state.shape[3]
    total_rows = 2 * rows_x * rows_y * lax.axis_size("gx") * lax.axis_size("gy")
    def temp_of(region):
        return 0.4 * state[(1,) + region].astype(jnp.float32) / state[(0,) + region].astype(jnp.float32)

    def shifted_pair(first, last, axis):
        count = lax.axis_size(axis)
        down = lax.ppermute(last, axis, [(i, i + 1) for i in range(count - 1)])
        up = lax.ppermute(first, axis, [(i + 1, i) for i in range(count - 1)])
        return down, up

    every = slice(None)
    top, bottom = shifted_pair(
        temp_of((every, slice(0, 2))), temp_of((every, slice(rows_x - 2, rows_x))), "gx"
    )
    slab = edges_of(state)
    count = lax.axis_size("gy")
    from_left = lax.ppermute(slab, "gy", [(i, i + 1) for i in range(count - 1)])
    from_right = lax.ppermute(slab, "gy", [(i + 1, i) for i in range(count - 1)])
    lane = lax.broadcasted_iota(jnp.int32, slab.shape, 2)
    xh = jnp.concatenate([top, bottom], axis=1)
    yh = jnp.where(lane % 4 < 2, from_left, from_right)
    half = snaps // 2
    contract = (((1, 2, 3), (1, 2, 3)), ((), ()))
    early = features_of(state, xh, yh, 0, 2)
    lead = lax.dot_general(
        early[:half], early[:half], contract, preferred_element_type=jnp.float32
    ) / total_rows
    lead = doubling_sum(doubling_sum(lead, "gx"), "gy")
    features = features_of(state, xh, yh, 1, 2, into=early)
    lower_rows = lax.dot_general(
        features[half:], features, contract, preferred_element_type=jnp.float32
    ) / total_rows
    lower_rows = doubling_sum(doubling_sum(lower_rows, "gx"), "gy")
    side = lower_rows[:, :half]
    corner = lower_rows[:, half:]
    gram = jnp.concatenate(
        [jnp.concatenate([lead, side.T], axis=1), lower_rows], axis=0
    )
    highest = lax.Precision.HIGHEST
    size = snaps - 1
    low11 = jnp.linalg.cholesky(lead)
    inv11 = tri_solve(low11, jnp.eye(half, dtype=jnp.float32))
    low21 = jnp.dot(side[: size - half], inv11.T, precision=highest)
    schur = corner[: size - half, : size - half] - jnp.dot(low21, low21.T, precision=highest)
    low22 = jnp.linalg.cholesky(schur)
    inv22 = tri_solve(low22, jnp.eye(size - half, dtype=jnp.float32))
    inv21 = -jnp.dot(inv22, jnp.dot(low21, inv11, precision=highest), precision=highest)
    inverse = jnp.concatenate(
        [
            jnp.concatenate([inv11, jnp.zeros((half, size - half), jnp.float32)], axis=1),
            jnp.concatenate([inv21, inv22], axis=1),
        ],
        axis=0,
    )
    cross = gram[:size, 1:]
    reduced = jnp.dot(jnp.dot(inverse, cross, precision=highest), inverse.T, precision=highest)
    shifted = jnp.concatenate(
        [jnp.zeros((snaps - 1, 1), jnp.bfloat16), inverse.astype(jnp.bfloat16)], axis=1
    )
    modes = lax.dot_general(
        shifted, features, (((1,), (0,)), ((), ())), preferred_element_type=jnp.float32
    ).astype(jnp.bfloat16)
    return (modes, reduced)


def solution(mesh):
    placed = (P(None, None, "gx", "gy"),)
    return jax.shard_map(
        shards,
        mesh=mesh,
        in_specs=placed,
        out_specs=(P(None, None, "gx", "gy"), P()),
        check_vma=False,
    )
```

```python
import jax
import jax.numpy as jnp
from jax import lax
from jax.experimental import pallas as pl
from jax.experimental.pallas import tpu as pltpu
from jax.sharding import PartitionSpec as P

BLOCK = 32


def feature_kernel(dens_ref, ener_ref, xh_ref, yh_ref, out_ref):
    nx = dens_ref.shape[2]
    ny = dens_ref.shape[3]
    lanes = yh_ref.shape[2]
    rows = lax.broadcasted_iota(jnp.int32, (nx, ny), 0)
    cols = lax.broadcasted_iota(jnp.int32, (nx, ny), 1)

    def body(s, carry):
        temp = 0.4 * ener_ref[0, s].astype(jnp.float32) / dens_ref[0, s].astype(jnp.float32)
        xh = xh_ref[s]
        halo = pltpu.roll(yh_ref[0], (ny - 2 - 4 * s) % lanes, 1)
        up2 = jnp.where(rows == 0, xh[0:1], jnp.where(rows == 1, xh[1:2], pltpu.roll(temp, 2, 0)))
        up1 = jnp.where(rows == 0, xh[1:2], pltpu.roll(temp, 1, 0))
        dn1 = jnp.where(rows == nx - 1, xh[2:3], pltpu.roll(temp, nx - 1, 0))
        dn2 = jnp.where(rows == nx - 2, xh[2:3], jnp.where(rows == nx - 1, xh[3:4], pltpu.roll(temp, nx - 2, 0)))
        lf2 = pltpu.roll(jnp.where(cols >= ny - 2, halo, temp), 2, 1)
        lf1 = pltpu.roll(jnp.where(cols == ny - 1, halo, temp), 1, 1)
        rt1 = pltpu.roll(jnp.where(cols == 0, halo, temp), ny - 1, 1)
        rt2 = pltpu.roll(jnp.where(cols < 2, halo, temp), ny - 2, 1)
        grad_x = (up2 - 8.0 * up1 + 8.0 * dn1 - dn2) / 12.0
        grad_y = (lf2 - 8.0 * lf1 + 8.0 * rt1 - rt2) / 12.0
        out_ref[s, 0] = grad_x.astype(out_ref.dtype)
        out_ref[s, 1] = grad_y.astype(out_ref.dtype)
        return carry

    lax.fori_loop(0, dens_ref.shape[1], body, 0, unroll=8)


def features_of(state, xh, yh):
    _, snaps, nx, ny = state.shape
    block = min(BLOCK, snaps)
    lanes = yh.shape[-1]
    return pl.pallas_call(
        feature_kernel,
        grid=(snaps // block,),
        in_specs=[
            pl.BlockSpec((1, block, nx, ny), lambda i: (0, i, 0, 0)),
            pl.BlockSpec((1, block, nx, ny), lambda i: (1, i, 0, 0)),
            pl.BlockSpec((block, 4, ny), lambda i: (i, 0, 0)),
            pl.BlockSpec((1, nx, lanes), lambda i: (i, 0, 0)),
        ],
        out_specs=pl.BlockSpec((block, 2, nx, ny), lambda i: (i, 0, 0, 0)),
        out_shape=jax.ShapeDtypeStruct((snaps, 2, nx, ny), jnp.bfloat16),
    )(state, state, xh, yh)


def edge_kernel(dens_ref, ener_ref, out_ref):
    nx = dens_ref.shape[2]
    ny = dens_ref.shape[3]
    group = lax.broadcasted_iota(jnp.int32, (nx, ny), 1) // 4

    def body(s, slab):
        temp = 0.4 * ener_ref[0, s].astype(jnp.float32) / dens_ref[0, s].astype(jnp.float32)
        return jnp.where(group == s, pltpu.roll(temp, (4 * s + 2) % ny, 1), slab)

    out_ref[0] = lax.fori_loop(0, dens_ref.shape[1], body, jnp.zeros((nx, ny), jnp.float32), unroll=8)


def edges_of(state):
    _, snaps, nx, ny = state.shape
    block = ny // 4
    return pl.pallas_call(
        edge_kernel,
        grid=(snaps // block,),
        in_specs=[
            pl.BlockSpec((1, block, nx, ny), lambda i: (0, i, 0, 0)),
            pl.BlockSpec((1, block, nx, ny), lambda i: (1, i, 0, 0)),
        ],
        out_specs=pl.BlockSpec((1, nx, ny), lambda i: (i, 0, 0)),
        out_shape=jax.ShapeDtypeStruct((snaps // block, nx, ny), jnp.float32),
    )(state, state)


def pack_symmetric(gram):
    half = gram.shape[0] // 2
    upper_left = gram[:half, :half]
    lower_right = gram[half:, half:]
    rows = lax.broadcasted_iota(jnp.int32, (half, half), 0)
    cols = lax.broadcasted_iota(jnp.int32, (half, half), 1)
    folded = jnp.where(rows >= cols, upper_left, lower_right)
    return jnp.concatenate(
        [gram[half:, :half], folded, jnp.diagonal(lower_right)[None]], axis=0
    )


def unpack_symmetric(packed):
    half = packed.shape[1]
    block = packed[:half]
    folded = packed[half : 2 * half]
    diag = packed[2 * half]
    rows = lax.broadcasted_iota(jnp.int32, (half, half), 0)
    cols = lax.broadcasted_iota(jnp.int32, (half, half), 1)
    upper_left = jnp.where(rows >= cols, folded, folded.T)
    lower_right = jnp.where(rows < cols, folded, folded.T)
    lower_right = jnp.where(rows == cols, diag[None, :], lower_right)
    return jnp.concatenate(
        [
            jnp.concatenate([upper_left, block.T], axis=1),
            jnp.concatenate([block, lower_right], axis=1),
        ],
        axis=0,
    )


def doubling_sum(value, axis, step=1, stop=None):
    count = lax.axis_size(axis)
    stop = count if stop is None else stop
    while step < stop:
        value = value + lax.ppermute(value, axis, [(i, i ^ step) for i in range(count)])
        step *= 2
    return value


def tri_solve(lower, right):
    return lax.linalg.triangular_solve(lower, right, left_side=True, lower=True)


def shards(state):
    snaps = state.shape[1]
    rows_x = state.shape[2]
    rows_y = state.shape[3]
    total_rows = 2 * rows_x * rows_y * lax.axis_size("gx") * lax.axis_size("gy")
    def temp_of(region):
        return 0.4 * state[(1,) + region].astype(jnp.float32) / state[(0,) + region].astype(jnp.float32)

    def shifted_pair(first, last, axis):
        count = lax.axis_size(axis)
        down = lax.ppermute(last, axis, [(i, i + 1) for i in range(count - 1)])
        up = lax.ppermute(first, axis, [(i + 1, i) for i in range(count - 1)])
        return down, up

    every = slice(None)
    top, bottom = shifted_pair(
        temp_of((every, slice(0, 2))), temp_of((every, slice(rows_x - 2, rows_x))), "gx"
    )
    slab = edges_of(state)
    count = lax.axis_size("gy")
    from_left = lax.ppermute(slab, "gy", [(i, i + 1) for i in range(count - 1)])
    from_right = lax.ppermute(slab, "gy", [(i + 1, i) for i in range(count - 1)])
    lane = lax.broadcasted_iota(jnp.int32, slab.shape, 2)
    features = features_of(
        state,
        jnp.concatenate([top, bottom], axis=1),
        jnp.where(lane % 4 < 2, from_left, from_right),
    )
    local_gram = (
        lax.dot_general(
            features, features, (((1, 2, 3), (1, 2, 3)), ((), ())), preferred_element_type=jnp.float32
        )
        / total_rows
    )
    half = snaps // 2
    packed = pack_symmetric(local_gram)
    folded = doubling_sum(packed[half : 2 * half], "gx", 1, 4)
    edge = jnp.concatenate([packed[:half], packed[2 * half :]], axis=0)
    folded, edge = lax.optimization_barrier((folded, edge))
    folded = doubling_sum(doubling_sum(folded, "gx", 4), "gy")
    edge = doubling_sum(doubling_sum(edge, "gx"), "gy")
    side = edge[:half]
    gram = unpack_symmetric(jnp.concatenate([side, folded, edge[half:]], axis=0))
    lead = gram[:half, :half]
    corner = gram[half:, half:]
    highest = lax.Precision.HIGHEST
    size = snaps - 1
    low11 = jnp.linalg.cholesky(lead)
    inv11 = tri_solve(low11, jnp.eye(half, dtype=jnp.float32))
    low21 = jnp.dot(side[: size - half], inv11.T, precision=highest)
    schur = corner[: size - half, : size - half] - jnp.dot(low21, low21.T, precision=highest)
    low22 = jnp.linalg.cholesky(schur)
    inv22 = tri_solve(low22, jnp.eye(size - half, dtype=jnp.float32))
    inv21 = -jnp.dot(inv22, jnp.dot(low21, inv11, precision=highest), precision=highest)
    inverse = jnp.concatenate(
        [
            jnp.concatenate([inv11, jnp.zeros((half, size - half), jnp.float32)], axis=1),
            jnp.concatenate([inv21, inv22], axis=1),
        ],
        axis=0,
    )
    cross = gram[:size, 1:]
    reduced = jnp.dot(jnp.dot(inverse, cross, precision=highest), inverse.T, precision=highest)
    shifted = jnp.concatenate(
        [jnp.zeros((snaps - 1, 1), jnp.bfloat16), inverse.astype(jnp.bfloat16)], axis=1
    )
    modes = lax.dot_general(
        shifted, features, (((1,), (0,)), ((), ())), preferred_element_type=jnp.float32
    ).astype(jnp.bfloat16)
    return (modes, reduced)


def solution(mesh):
    placed = (P(None, None, "gx", "gy"),)
    return jax.shard_map(
        shards,
        mesh=mesh,
        in_specs=placed,
        out_specs=(P(None, None, "gx", "gy"), P()),
        check_vma=False,
    )
```

```python
import jax
import jax.numpy as jnp
from jax import lax
from jax.experimental import pallas as pl
from jax.experimental.pallas import tpu as pltpu
from jax.sharding import PartitionSpec as P

BLOCK = 32


def feature_kernel(dens_ref, ener_ref, xh_ref, yh_ref, out_ref):
    nx = dens_ref.shape[2]
    ny = dens_ref.shape[3]
    lanes = yh_ref.shape[2]
    rows = lax.broadcasted_iota(jnp.int32, (nx, ny), 0)
    cols = lax.broadcasted_iota(jnp.int32, (nx, ny), 1)

    def body(s, carry):
        temp = 0.4 * ener_ref[0, s].astype(jnp.float32) / dens_ref[0, s].astype(jnp.float32)
        xh = xh_ref[s]
        halo = pltpu.roll(yh_ref[0], (ny - 2 - 4 * s) % lanes, 1)
        up2 = jnp.where(rows == 0, xh[0:1], jnp.where(rows == 1, xh[1:2], pltpu.roll(temp, 2, 0)))
        up1 = jnp.where(rows == 0, xh[1:2], pltpu.roll(temp, 1, 0))
        dn1 = jnp.where(rows == nx - 1, xh[2:3], pltpu.roll(temp, nx - 1, 0))
        dn2 = jnp.where(rows == nx - 2, xh[2:3], jnp.where(rows == nx - 1, xh[3:4], pltpu.roll(temp, nx - 2, 0)))
        lf2 = pltpu.roll(jnp.where(cols >= ny - 2, halo, temp), 2, 1)
        lf1 = pltpu.roll(jnp.where(cols == ny - 1, halo, temp), 1, 1)
        rt1 = pltpu.roll(jnp.where(cols == 0, halo, temp), ny - 1, 1)
        rt2 = pltpu.roll(jnp.where(cols < 2, halo, temp), ny - 2, 1)
        grad_x = (up2 - 8.0 * up1 + 8.0 * dn1 - dn2) / 12.0
        grad_y = (lf2 - 8.0 * lf1 + 8.0 * rt1 - rt2) / 12.0
        out_ref[s, 0] = grad_x.astype(out_ref.dtype)
        out_ref[s, 1] = grad_y.astype(out_ref.dtype)
        return carry

    lax.fori_loop(0, dens_ref.shape[1], body, 0, unroll=8)


def features_of(state, xh, yh):
    _, snaps, nx, ny = state.shape
    block = min(BLOCK, snaps)
    lanes = yh.shape[-1]
    return pl.pallas_call(
        feature_kernel,
        grid=(snaps // block,),
        in_specs=[
            pl.BlockSpec((1, block, nx, ny), lambda i: (0, i, 0, 0)),
            pl.BlockSpec((1, block, nx, ny), lambda i: (1, i, 0, 0)),
            pl.BlockSpec((block, 4, ny), lambda i: (i, 0, 0)),
            pl.BlockSpec((1, nx, lanes), lambda i: (i, 0, 0)),
        ],
        out_specs=pl.BlockSpec((block, 2, nx, ny), lambda i: (i, 0, 0, 0)),
        out_shape=jax.ShapeDtypeStruct((snaps, 2, nx, ny), jnp.bfloat16),
    )(state, state, xh, yh)


def edge_kernel(dens_ref, ener_ref, out_ref):
    nx = dens_ref.shape[2]
    ny = dens_ref.shape[3]
    group = lax.broadcasted_iota(jnp.int32, (nx, ny), 1) // 4

    def body(s, slabs):
        shift = (4 * s + 2) % ny
        dens = pltpu.roll(dens_ref[0, s].astype(jnp.float32), shift, 1)
        ener = pltpu.roll(ener_ref[0, s].astype(jnp.float32), shift, 1)
        return jnp.where(group == s, dens, slabs[0]), jnp.where(group == s, ener, slabs[1])

    ones = jnp.ones((nx, ny), jnp.float32)
    dens, ener = lax.fori_loop(0, dens_ref.shape[1], body, (ones, ones), unroll=8)
    out_ref[0] = 0.4 * ener / dens


def edges_of(state):
    _, snaps, nx, ny = state.shape
    block = ny // 4
    return pl.pallas_call(
        edge_kernel,
        grid=(snaps // block,),
        in_specs=[
            pl.BlockSpec((1, block, nx, ny), lambda i: (0, i, 0, 0)),
            pl.BlockSpec((1, block, nx, ny), lambda i: (1, i, 0, 0)),
        ],
        out_specs=pl.BlockSpec((1, nx, ny), lambda i: (i, 0, 0)),
        out_shape=jax.ShapeDtypeStruct((snaps // block, nx, ny), jnp.float32),
    )(state, state)


def pack_symmetric(gram):
    half = gram.shape[0] // 2
    upper_left = gram[:half, :half]
    lower_right = gram[half:, half:]
    rows = lax.broadcasted_iota(jnp.int32, (half, half), 0)
    cols = lax.broadcasted_iota(jnp.int32, (half, half), 1)
    folded = jnp.where(rows >= cols, upper_left, lower_right)
    return jnp.concatenate(
        [gram[half:, :half], folded, jnp.diagonal(lower_right)[None]], axis=0
    )


def unpack_symmetric(packed):
    half = packed.shape[1]
    block = packed[:half]
    folded = packed[half : 2 * half]
    diag = packed[2 * half]
    rows = lax.broadcasted_iota(jnp.int32, (half, half), 0)
    cols = lax.broadcasted_iota(jnp.int32, (half, half), 1)
    upper_left = jnp.where(rows >= cols, folded, folded.T)
    lower_right = jnp.where(rows < cols, folded, folded.T)
    lower_right = jnp.where(rows == cols, diag[None, :], lower_right)
    return jnp.concatenate(
        [
            jnp.concatenate([upper_left, block.T], axis=1),
            jnp.concatenate([block, lower_right], axis=1),
        ],
        axis=0,
    )


def doubling_sum(value, axis):
    count = lax.axis_size(axis)
    step = 1
    while step < count:
        value = value + lax.ppermute(value, axis, [(i, i ^ step) for i in range(count)])
        step *= 2
    return value


def tri_solve(lower, right):
    return lax.linalg.triangular_solve(lower, right, left_side=True, lower=True)


def shards(state):
    snaps = state.shape[1]
    rows_x = state.shape[2]
    rows_y = state.shape[3]
    total_rows = 2 * rows_x * rows_y * lax.axis_size("gx") * lax.axis_size("gy")
    def temp_of(region):
        return 0.4 * state[(1,) + region].astype(jnp.float32) / state[(0,) + region].astype(jnp.float32)

    def shifted_pair(first, last, axis):
        count = lax.axis_size(axis)
        down = lax.ppermute(last, axis, [(i, i + 1) for i in range(count - 1)])
        up = lax.ppermute(first, axis, [(i + 1, i) for i in range(count - 1)])
        return down, up

    every = slice(None)
    top, bottom = shifted_pair(
        temp_of((every, slice(0, 2))), temp_of((every, slice(rows_x - 2, rows_x))), "gx"
    )
    slab = edges_of(state)
    count = lax.axis_size("gy")
    from_left = lax.ppermute(slab, "gy", [(i, i + 1) for i in range(count - 1)])
    from_right = lax.ppermute(slab, "gy", [(i + 1, i) for i in range(count - 1)])
    lane = lax.broadcasted_iota(jnp.int32, slab.shape, 2)
    features = features_of(
        state,
        jnp.concatenate([top, bottom], axis=1),
        jnp.where(lane % 4 < 2, from_left, from_right),
    )
    local_gram = (
        lax.dot_general(
            features, features, (((1, 2, 3), (1, 2, 3)), ((), ())), preferred_element_type=jnp.float32
        )
        / total_rows
    )
    half = snaps // 2
    packed = pack_symmetric(local_gram)
    folded = doubling_sum(doubling_sum(packed[half : 2 * half], "gx"), "gy")
    edge = jnp.concatenate([packed[:half], packed[2 * half :]], axis=0)
    edge = doubling_sum(doubling_sum(edge, "gx"), "gy")
    side = edge[:half]
    gram = unpack_symmetric(jnp.concatenate([side, folded, edge[half:]], axis=0))
    lead = gram[:half, :half]
    corner = gram[half:, half:]
    highest = lax.Precision.HIGHEST
    size = snaps - 1
    low11 = jnp.linalg.cholesky(lead)
    inv11 = tri_solve(low11, jnp.eye(half, dtype=jnp.float32))
    low21 = jnp.dot(side[: size - half], inv11.T, precision=highest)
    schur = corner[: size - half, : size - half] - jnp.dot(low21, low21.T, precision=highest)
    low22 = jnp.linalg.cholesky(schur)
    inv22 = tri_solve(low22, jnp.eye(size - half, dtype=jnp.float32))
    inv21 = -jnp.dot(inv22, jnp.dot(low21, inv11, precision=highest), precision=highest)
    inverse = jnp.concatenate(
        [
            jnp.concatenate([inv11, jnp.zeros((half, size - half), jnp.float32)], axis=1),
            jnp.concatenate([inv21, inv22], axis=1),
        ],
        axis=0,
    )
    cross = gram[:size, 1:]
    reduced = jnp.dot(jnp.dot(inverse, cross, precision=highest), inverse.T, precision=highest)
    shifted = jnp.concatenate(
        [jnp.zeros((snaps - 1, 1), jnp.bfloat16), inverse.astype(jnp.bfloat16)], axis=1
    )
    modes = lax.dot_general(
        shifted, features, (((1,), (0,)), ((), ())), preferred_element_type=jnp.float32
    ).astype(jnp.bfloat16)
    return (modes, reduced)


def solution(mesh):
    placed = (P(None, None, "gx", "gy"),)
    return jax.shard_map(
        shards,
        mesh=mesh,
        in_specs=placed,
        out_specs=(P(None, None, "gx", "gy"), P()),
        check_vma=False,
    )
```

```python
import jax
import jax.numpy as jnp
from jax import lax
from jax.experimental import pallas as pl
from jax.experimental.pallas import tpu as pltpu
from jax.sharding import PartitionSpec as P

BLOCK = 32


def feature_kernel(dens_ref, ener_ref, xh_ref, yh_ref, out_ref):
    nx = dens_ref.shape[2]
    ny = dens_ref.shape[3]
    lanes = yh_ref.shape[2]
    rows = lax.broadcasted_iota(jnp.int32, (nx, ny), 0)
    src = lax.broadcasted_iota(jnp.int32, (ny, ny), 0)
    dst = lax.broadcasted_iota(jnp.int32, (ny, ny), 1)
    gap = src - dst
    inner = jnp.where(gap == -2, 1.0, 0.0) - jnp.where(gap == -1, 8.0, 0.0)
    inner = inner + jnp.where(gap == 1, 8.0, 0.0) - jnp.where(gap == 2, 1.0, 0.0)

    def tap(i, j, value):
        return jnp.where((src == i) & (dst == j), value, 0.0)

    outer = tap(ny - 2, 0, 1.0) + tap(ny - 1, 0, -8.0) + tap(ny - 1, 1, 1.0)
    outer = outer + tap(0, ny - 2, -1.0) + tap(0, ny - 1, 8.0) + tap(1, ny - 1, -1.0)
    stencil = jnp.concatenate([inner, outer], axis=0)

    def body(s, carry):
        temp = 0.4 * ener_ref[0, s].astype(jnp.float32) / dens_ref[0, s].astype(jnp.float32)
        xh = xh_ref[s]
        halo = pltpu.roll(yh_ref[0], (ny - 2 - 4 * s) % lanes, 1)
        up2 = jnp.where(rows == 0, xh[0:1], jnp.where(rows == 1, xh[1:2], pltpu.roll(temp, 2, 0)))
        up1 = jnp.where(rows == 0, xh[1:2], pltpu.roll(temp, 1, 0))
        dn1 = jnp.where(rows == nx - 1, xh[2:3], pltpu.roll(temp, nx - 1, 0))
        dn2 = jnp.where(rows == nx - 2, xh[2:3], jnp.where(rows == nx - 1, xh[3:4], pltpu.roll(temp, nx - 2, 0)))
        grad_x = (up2 - 8.0 * up1 + 8.0 * dn1 - dn2) / 12.0
        grad_y = jnp.dot(
            jnp.concatenate([temp, halo], axis=1),
            stencil,
            precision=lax.Precision.HIGHEST,
            preferred_element_type=jnp.float32,
        ) / 12.0
        out_ref[s, 0] = grad_x.astype(out_ref.dtype)
        out_ref[s, 1] = grad_y.astype(out_ref.dtype)
        return carry

    lax.fori_loop(0, dens_ref.shape[1], body, 0, unroll=8)


def features_of(state, xh, yh):
    _, snaps, nx, ny = state.shape
    block = min(BLOCK, snaps)
    lanes = yh.shape[-1]
    return pl.pallas_call(
        feature_kernel,
        grid=(snaps // block,),
        in_specs=[
            pl.BlockSpec((1, block, nx, ny), lambda i: (0, i, 0, 0)),
            pl.BlockSpec((1, block, nx, ny), lambda i: (1, i, 0, 0)),
            pl.BlockSpec((block, 4, ny), lambda i: (i, 0, 0)),
            pl.BlockSpec((1, nx, lanes), lambda i: (i, 0, 0)),
        ],
        out_specs=pl.BlockSpec((block, 2, nx, ny), lambda i: (i, 0, 0, 0)),
        out_shape=jax.ShapeDtypeStruct((snaps, 2, nx, ny), jnp.bfloat16),
    )(state, state, xh, yh)


def edge_kernel(dens_ref, ener_ref, out_ref):
    nx = dens_ref.shape[2]
    ny = dens_ref.shape[3]
    group = lax.broadcasted_iota(jnp.int32, (nx, ny), 1) // 4

    def body(s, slab):
        temp = 0.4 * ener_ref[0, s].astype(jnp.float32) / dens_ref[0, s].astype(jnp.float32)
        return jnp.where(group == s, pltpu.roll(temp, (4 * s + 2) % ny, 1), slab)

    out_ref[0] = lax.fori_loop(0, dens_ref.shape[1], body, jnp.zeros((nx, ny), jnp.float32), unroll=8)


def edges_of(state):
    _, snaps, nx, ny = state.shape
    block = ny // 4
    return pl.pallas_call(
        edge_kernel,
        grid=(snaps // block,),
        in_specs=[
            pl.BlockSpec((1, block, nx, ny), lambda i: (0, i, 0, 0)),
            pl.BlockSpec((1, block, nx, ny), lambda i: (1, i, 0, 0)),
        ],
        out_specs=pl.BlockSpec((1, nx, ny), lambda i: (i, 0, 0)),
        out_shape=jax.ShapeDtypeStruct((snaps // block, nx, ny), jnp.float32),
    )(state, state)


def pack_symmetric(gram):
    half = gram.shape[0] // 2
    upper_left = gram[:half, :half]
    lower_right = gram[half:, half:]
    rows = lax.broadcasted_iota(jnp.int32, (half, half), 0)
    cols = lax.broadcasted_iota(jnp.int32, (half, half), 1)
    folded = jnp.where(rows >= cols, upper_left, lower_right)
    return jnp.concatenate(
        [gram[half:, :half], folded, jnp.diagonal(lower_right)[None]], axis=0
    )


def unpack_symmetric(packed):
    half = packed.shape[1]
    block = packed[:half]
    folded = packed[half : 2 * half]
    diag = packed[2 * half]
    rows = lax.broadcasted_iota(jnp.int32, (half, half), 0)
    cols = lax.broadcasted_iota(jnp.int32, (half, half), 1)
    upper_left = jnp.where(rows >= cols, folded, folded.T)
    lower_right = jnp.where(rows < cols, folded, folded.T)
    lower_right = jnp.where(rows == cols, diag[None, :], lower_right)
    return jnp.concatenate(
        [
            jnp.concatenate([upper_left, block.T], axis=1),
            jnp.concatenate([block, lower_right], axis=1),
        ],
        axis=0,
    )


def doubling_sum(value, axis):
    count = lax.axis_size(axis)
    step = 1
    while step < count:
        value = value + lax.ppermute(value, axis, [(i, i ^ step) for i in range(count)])
        step *= 2
    return value


def tri_solve(lower, right):
    return lax.linalg.triangular_solve(lower, right, left_side=True, lower=True)


def shards(state):
    snaps = state.shape[1]
    rows_x = state.shape[2]
    rows_y = state.shape[3]
    total_rows = 2 * rows_x * rows_y * lax.axis_size("gx") * lax.axis_size("gy")
    def temp_of(region):
        return 0.4 * state[(1,) + region].astype(jnp.float32) / state[(0,) + region].astype(jnp.float32)

    def shifted_pair(first, last, axis):
        count = lax.axis_size(axis)
        down = lax.ppermute(last, axis, [(i, i + 1) for i in range(count - 1)])
        up = lax.ppermute(first, axis, [(i + 1, i) for i in range(count - 1)])
        return down, up

    every = slice(None)
    top, bottom = shifted_pair(
        temp_of((every, slice(0, 2))), temp_of((every, slice(rows_x - 2, rows_x))), "gx"
    )
    slab = edges_of(state)
    count = lax.axis_size("gy")
    from_left = lax.ppermute(slab, "gy", [(i, i + 1) for i in range(count - 1)])
    from_right = lax.ppermute(slab, "gy", [(i + 1, i) for i in range(count - 1)])
    lane = lax.broadcasted_iota(jnp.int32, slab.shape, 2)
    features = features_of(
        state,
        jnp.concatenate([top, bottom], axis=1),
        jnp.where(lane % 4 < 2, from_left, from_right),
    )
    local_gram = (
        lax.dot_general(
            features, features, (((1, 2, 3), (1, 2, 3)), ((), ())), preferred_element_type=jnp.float32
        )
        / total_rows
    )
    half = snaps // 2
    packed = pack_symmetric(local_gram)
    folded = doubling_sum(doubling_sum(packed[half : 2 * half], "gx"), "gy")
    edge = jnp.concatenate([packed[:half], packed[2 * half :]], axis=0)
    edge = doubling_sum(doubling_sum(edge, "gx"), "gy")
    side = edge[:half]
    gram = unpack_symmetric(jnp.concatenate([side, folded, edge[half:]], axis=0))
    lead = gram[:half, :half]
    corner = gram[half:, half:]
    highest = lax.Precision.HIGHEST
    size = snaps - 1
    low11 = jnp.linalg.cholesky(lead)
    inv11 = tri_solve(low11, jnp.eye(half, dtype=jnp.float32))
    low21 = jnp.dot(side[: size - half], inv11.T, precision=highest)
    schur = corner[: size - half, : size - half] - jnp.dot(low21, low21.T, precision=highest)
    low22 = jnp.linalg.cholesky(schur)
    inv22 = tri_solve(low22, jnp.eye(size - half, dtype=jnp.float32))
    inv21 = -jnp.dot(inv22, jnp.dot(low21, inv11, precision=highest), precision=highest)
    inverse = jnp.concatenate(
        [
            jnp.concatenate([inv11, jnp.zeros((half, size - half), jnp.float32)], axis=1),
            jnp.concatenate([inv21, inv22], axis=1),
        ],
        axis=0,
    )
    cross = gram[:size, 1:]
    reduced = jnp.dot(jnp.dot(inverse, cross, precision=highest), inverse.T, precision=highest)
    shifted = jnp.concatenate(
        [jnp.zeros((snaps - 1, 1), jnp.bfloat16), inverse.astype(jnp.bfloat16)], axis=1
    )
    modes = lax.dot_general(
        shifted, features, (((1,), (0,)), ((), ())), preferred_element_type=jnp.float32
    ).astype(jnp.bfloat16)
    return (modes, reduced)


def solution(mesh):
    placed = (P(None, None, "gx", "gy"),)
    return jax.shard_map(
        shards,
        mesh=mesh,
        in_specs=placed,
        out_specs=(P(None, None, "gx", "gy"), P()),
        check_vma=False,
    )
```
